1024 devices in a mesh: seq: 32 (over z_lo, y), head: 32 (over z_hi, x, core).
Axes of the slice: x: 4, y: 4, z: 32 (z_hi: 4, z_lo: 8; z = z_hi * 8 + z_lo), core: 2. Of those that a mesh axis runs over, the one named last changes fastest.
Arguments:
- query: bfloat16 [8192, 4096], P('seq', 'head'), may hold values from -131 to 131
- keys: bfloat16 [8192, 4096], P('seq', 'head'), may hold values from -5 to 5, as said below
- values: bfloat16 [8192, 4096], P('seq', 'head'), may hold values from -5 to 5, as said below
- d_out: bfloat16 [8192, 5376], P('seq', 'head'), may hold values from -6 to 6
- w_out: bfloat16 [4096, 5376], P('head'), may hold values from -0.09375 to 0.09375
- w_query: bfloat16 [5376, 4096], P(None, 'head'), may hold values from -0.078125 to 0.078125
- w_key: bfloat16 [5376, 4096], P(None, 'head'), as said below
- w_value: bfloat16 [5376, 4096], P(None, 'head'), as said below
Outputs:
- grad_input: bfloat16 [8192, 5376], P('seq', 'head')
The draws below stay inside these ranges and needn't reach their ends.
Inputs may be any that keep to these rules, and one draw needn't show every extreme that they name: `keys`: the columns of query heads 2i and 2i + 1 are equal: both read key head i. `values`: the columns of query heads 2i and 2i + 1 are equal: both read value head i. `w_key`: the columns of query heads 2i and 2i + 1 are equal; every entry lies within 5 / sqrt(5376) in magnitude. `w_value`: the columns of query heads 2i and 2i + 1 are equal; every entry lies within 5 / sqrt(5376) in magnitude.
All inputs are finite; a program needn't handle non-finite values.
Results may differ from the reference program's by a relative error of at most 0.03.
Values may be sent and summed in bfloat16 or wider, within the bound.
No kernel may reach another device: no remote copies, remote signals or barrier semaphores. Data moves between devices by JAX's collectives and lax.ppermute only.
A program may use at most 32 MiB of HBM per device.

```python
import jax
import jax.numpy as jnp
from jax import lax

D = 5376
HEAD_DIM = 128
WINDOW = 1024
TOK_DEV = 256
QHEADS = 32
KVHEADS = 16
TOKENS = 8192
NBR = 4


def shared_keys(key):
    return jax.random.truncated_normal(jax.random.fold_in(key, 101), -5.0, 5.0, (TOKENS, KVHEADS, HEAD_DIM), jnp.float32)


def paired(fields, leading):
    return jnp.repeat(fields, 2, axis=1).reshape(leading, QHEADS * HEAD_DIM).astype(jnp.bfloat16)


def draw_query(key, part):
    queries = jax.random.truncated_normal(jax.random.fold_in(key, 102), -5.0, 5.0, (TOKENS, QHEADS, HEAD_DIM), jnp.float32)
    return queries.reshape(TOKENS, QHEADS * HEAD_DIM).astype(jnp.bfloat16)


def draw_keys(key, part):
    fields = shared_keys(key)
    return paired(fields, TOKENS)


def draw_values(key, part):
    fields = jax.random.truncated_normal(jax.random.fold_in(key, 104), -5.0, 5.0, (TOKENS, KVHEADS, HEAD_DIM), jnp.float32)
    return paired(fields, TOKENS)


def draw_w_key(key, part):
    fields = jax.random.truncated_normal(jax.random.fold_in(key, 105), -5.0, 5.0, (D, KVHEADS, HEAD_DIM), jnp.float32)
    return paired(fields * D ** (-0.5), D)


def draw_w_value(key, part):
    fields = jax.random.truncated_normal(jax.random.fold_in(key, 106), -5.0, 5.0, (D, KVHEADS, HEAD_DIM), jnp.float32)
    return paired(fields * D ** (-0.5), D)


def block_scale(key, shape, pieces, low, high):
    level = 1.0
    for dim, blocks in pieces:
        draws = jax.random.uniform(jax.random.fold_in(jax.random.fold_in(key, 6), dim), (blocks,), jnp.float32, low / len(pieces), high / len(pieces))
        level = level * jnp.repeat(jnp.exp(draws), shape[dim] // blocks).reshape((-1,) + (1,) * (len(shape) - 1 - dim))
    return level


def centred(rng, extent, deviation, bound, split=(), kind=jnp.bfloat16):
    result = deviation * jax.random.normal(rng, extent, jnp.float32)
    if split:
        result = result * block_scale(rng, extent, split, -0.22, 0.18)
    return jnp.clip(result, -bound, bound).astype(kind)


def setup_inputs(seed: int = 0) -> dict:
    seeds = jax.random.split(jax.random.key(seed), 9)
    query = draw_query(jax.random.fold_in(seeds[8], 71), 0)
    keys = draw_keys(jax.random.fold_in(seeds[8], 71), 0)
    values = draw_values(jax.random.fold_in(seeds[8], 71), 0)
    d_out = centred(seeds[3], (TOKENS, D), 1.0, 6.0, ((0, 32), (1, 32)))
    w_out = centred(seeds[4], (QHEADS * HEAD_DIM, D), (QHEADS * HEAD_DIM) ** -0.5, 0.09375, ((0, 32),))
    w_query = centred(seeds[5], (D, QHEADS * HEAD_DIM), D ** -0.5, 0.078125, ((1, 32),))
    w_key = draw_w_key(jax.random.fold_in(seeds[8], 71), 0)
    w_value = draw_w_value(jax.random.fold_in(seeds[8], 71), 0)
    return {"query": query, "keys": keys, "values": values, "d_out": d_out, "w_out": w_out, "w_query": w_query, "w_key": w_key, "w_value": w_value}


score_scale = 168.0 ** -0.5


def dot_rows(left, right):
    return lax.dot_general(left, right, (((1,), (1,)), ((), ())), preferred_element_type=jnp.float32)


def dot_cols(left, right):
    return lax.dot_general(left, right, (((0,), (0,)), ((), ())), preferred_element_type=jnp.float32)


def band_backward(query_block, key_band, value_band, grad_block, query_start, key_start):
    length = query_block.shape[0]
    span = key_band.shape[0]
    query_pos = query_start + jnp.arange(length, dtype=jnp.int32)
    key_pos = key_start + jnp.arange(span, dtype=jnp.int32)
    offset = query_pos[:, None] - key_pos[None, :]
    allowed = (key_pos[None, :] >= 0) & (offset >= 0) & (offset < WINDOW)
    scores = dot_rows(query_block, key_band) * score_scale
    masked = jnp.where(allowed, scores, -1e30)
    top = jnp.max(masked, axis=1, keepdims=True)
    weights = jnp.where(allowed, jnp.exp(masked - top), 0.0)
    probs = weights / jnp.sum(weights, axis=1, keepdims=True)
    probs_low = probs.astype(jnp.bfloat16)
    grad_probs = dot_rows(grad_block, value_band)
    delta = jnp.sum(probs * grad_probs, axis=1, keepdims=True)
    grad_scores = (probs * (grad_probs - delta)).astype(jnp.bfloat16)
    grad_query = (jnp.dot(grad_scores, key_band, preferred_element_type=jnp.float32) * score_scale).astype(jnp.bfloat16)
    grad_keys = (dot_cols(grad_scores, query_block) * score_scale).astype(jnp.bfloat16)
    grad_values = dot_cols(probs_low, grad_block).astype(jnp.bfloat16)
    return grad_query, grad_keys, grad_values


def head_grads(query_head, keys_head, values_head, grad_head):
    reach = NBR
    span = (reach + 1) * TOK_DEV
    blocks = TOKENS // TOK_DEV
    padding = jnp.zeros((reach * TOK_DEV, HEAD_DIM), keys_head.dtype)
    key_padded = jnp.concatenate([padding, keys_head], axis=0)
    value_padded = jnp.concatenate([padding, values_head], axis=0)

    def one_block(index):
        start = index * TOK_DEV
        query_block = lax.dynamic_slice_in_dim(query_head, start, TOK_DEV, 0)
        grad_block = lax.dynamic_slice_in_dim(grad_head, start, TOK_DEV, 0)
        key_band = lax.dynamic_slice_in_dim(key_padded, start, span, 0)
        value_band = lax.dynamic_slice_in_dim(value_padded, start, span, 0)
        return band_backward(query_block, key_band, value_band, grad_block, start, start - reach * TOK_DEV)

    grad_query, key_parts, value_parts = lax.map(one_block, jnp.arange(blocks, dtype=jnp.int32))
    grad_query = grad_query.reshape(TOKENS, HEAD_DIM)

    def assemble(parts):
        parts = parts.reshape(blocks, reach + 1, TOK_DEV, HEAD_DIM).astype(jnp.float32)
        summed = jnp.zeros(((blocks + reach) * TOK_DEV, HEAD_DIM), jnp.float32)
        for offset in range(reach + 1):
            piece = parts[:, offset].reshape(TOKENS, HEAD_DIM)
            summed = summed + jnp.pad(piece, ((offset * TOK_DEV, (reach - offset) * TOK_DEV), (0, 0)))
        return summed[reach * TOK_DEV:].astype(jnp.bfloat16)

    return grad_query, assemble(key_parts), assemble(value_parts)


def reference(query, keys, values, d_out, w_out, w_query, w_key, w_value):
    def one_head(carried, head):
        first = head * HEAD_DIM
        query_head = lax.dynamic_slice_in_dim(query, first, HEAD_DIM, 1)
        keys_head = lax.dynamic_slice_in_dim(keys, first, HEAD_DIM, 1)
        values_head = lax.dynamic_slice_in_dim(values, first, HEAD_DIM, 1)
        out_rows = lax.dynamic_slice_in_dim(w_out, first, HEAD_DIM, 0)
        grad_head = dot_rows(d_out, out_rows).astype(jnp.bfloat16)
        grad_query, grad_keys, grad_values = head_grads(query_head, keys_head, values_head, grad_head)
        term = dot_rows(grad_query, lax.dynamic_slice_in_dim(w_query, first, HEAD_DIM, 1))
        term = term + dot_rows(grad_keys, lax.dynamic_slice_in_dim(w_key, first, HEAD_DIM, 1))
        term = term + dot_rows(grad_values, lax.dynamic_slice_in_dim(w_value, first, HEAD_DIM, 1))
        rounded = lax.optimization_barrier(term.astype(jnp.bfloat16))
        return carried + rounded.astype(jnp.float32), None

    start_total = jnp.zeros((TOKENS, D), jnp.float32)
    summed, unused = lax.scan(one_head, start_total, jnp.arange(QHEADS, dtype=jnp.int32))
    return summed.astype(jnp.bfloat16)
```

```python
import jax
import jax.numpy as jnp
from jax import lax
from jax.sharding import Mesh
from jax.sharding import PartitionSpec as P

WINDOW = 1024
NBR = 4


score_scale = 168.0 ** (-0.5)


def from_behind(block, axis, distance):
    devices = range(lax.axis_size(axis))
    route = [(i - distance, i) for i in devices if i - distance in devices]
    return lax.ppermute(block, axis, route)


def shift(block, axis, size, step):
    return lax.ppermute(block, axis, [(i, (i + step) % size) for i in range(size)])


def gather_axis(block, axis, size):
    me = lax.axis_index(axis)
    buf = jnp.zeros((size,) + block.shape, block.dtype)
    buf = lax.dynamic_update_index_in_dim(buf, block, me, 0)
    for step in range(1, size):
        got = shift(block, axis, size, step)
        buf = lax.dynamic_update_index_in_dim(buf, got, (me - step) % size, 0)
    return buf


def scatter_axis(parts, axis, size, dim):
    me = lax.axis_index(axis)
    acc = lax.dynamic_index_in_dim(parts, me, dim, keepdims=False).astype(jnp.float32)
    for step in range(1, size):
        out = lax.dynamic_index_in_dim(parts, (me + step) % size, dim, keepdims=False)
        acc = acc + shift(out.astype(jnp.bfloat16), axis, size, step).astype(jnp.float32)
    return acc


def dot_rows(left, right):
    return lax.dot_general(
        left, right, (((1,), (1,)), ((), ())), preferred_element_type=jnp.float32
    )


def dot_cols(left, right):
    return lax.dot_general(
        left, right, (((0,), (0,)), ((), ())), preferred_element_type=jnp.float32
    )


def band_backward(query_block, key_band, value_band, grad_block, query_start, key_start):
    length = query_block.shape[0]
    span = key_band.shape[0]
    query_pos = query_start + jnp.arange(length, dtype=jnp.int32)
    key_pos = key_start + jnp.arange(span, dtype=jnp.int32)
    offset = query_pos[:, None] - key_pos[None, :]
    allowed = (key_pos[None, :] >= 0) & (offset >= 0) & (offset < WINDOW)
    scores = dot_rows(query_block, key_band) * score_scale
    masked = jnp.where(allowed, scores, -1e30)
    top = jnp.max(masked, axis=1, keepdims=True)
    weights = jnp.where(allowed, jnp.exp(masked - top), 0.0)
    probs = weights / jnp.sum(weights, axis=1, keepdims=True)
    probs_low = probs.astype(jnp.bfloat16)
    grad_probs = dot_rows(grad_block, value_band)
    delta = jnp.sum(probs * grad_probs, axis=1, keepdims=True)
    grad_scores = (probs * (grad_probs - delta)).astype(jnp.bfloat16)
    grad_query = (
        jnp.dot(grad_scores, key_band, preferred_element_type=jnp.float32) * score_scale
    ).astype(jnp.bfloat16)
    grad_keys = (dot_cols(grad_scores, query_block) * score_scale).astype(jnp.bfloat16)
    grad_values = dot_cols(probs_low, grad_block).astype(jnp.bfloat16)
    return (grad_query, grad_keys, grad_values)


def make_body(n_zhi, n_x, n_core):
    def body(query, keys, values, d_out, w_out, w_query, w_key, w_value):
        length, dim = query.shape
        width = d_out.shape[1]
        seq_index = lax.axis_index("seq")
        stacked = gather_axis(d_out, "zhi", n_zhi)
        stacked = gather_axis(stacked, "x", n_x)
        stacked = gather_axis(stacked, "core", n_core)
        out_rows = w_out.reshape(w_out.shape[0], n_zhi, n_x, n_core, width)
        grad_heads = jnp.einsum(
            "cxzti,hzxci->th", stacked, out_rows, preferred_element_type=jnp.float32
        ).astype(jnp.bfloat16)
        reach = NBR
        kv = jnp.concatenate([keys, values], axis=1)
        kv_blocks = [from_behind(kv, "seq", distance) for distance in range(reach, 0, -1)]
        kv_band = jnp.concatenate(kv_blocks + [kv], axis=0)
        key_band = kv_band[:, :dim]
        value_band = kv_band[:, dim:]
        query_start = seq_index * length
        grad_query, key_parts, value_parts = band_backward(
            query, key_band, value_band, grad_heads, query_start, query_start - reach * length
        )
        kv_parts = jnp.concatenate([key_parts, value_parts], axis=1)
        kv_total = kv_parts[reach * length :].astype(jnp.float32)
        for distance in range(1, reach + 1):
            first = (reach - distance) * length
            back = from_behind(kv_parts[first : first + length], "seq", -distance)
            kv_total = kv_total + back.astype(jnp.float32)
        kv_total = kv_total.astype(jnp.bfloat16)
        grad_keys = kv_total[:, :dim]
        grad_values = kv_total[:, dim:]
        summed = dot_rows(w_query, grad_query)
        summed = summed + dot_rows(w_key, grad_keys)
        summed = summed + dot_rows(w_value, grad_values)
        term = summed.astype(jnp.bfloat16).reshape(n_zhi, n_x, n_core, width, length)
        part = scatter_axis(term, "core", n_core, 2)
        part = scatter_axis(part, "x", n_x, 1)
        part = scatter_axis(part, "zhi", n_zhi, 0)
        return part.T.astype(jnp.bfloat16)

    return body


def solution(mesh):
    n_seq, n_head = mesh.devices.shape
    n_core = 2
    n_x = len({d.coords[0] for d in mesh.devices[0]})
    n_zhi = n_head // (n_x * n_core)
    fine = Mesh(mesh.devices.reshape(n_seq, n_zhi, n_x, n_core), ("seq", "zhi", "x", "core"))
    head = ("zhi", "x", "core")
    in_specs = (
        P("seq", head),
        P("seq", head),
        P("seq", head),
        P("seq", head),
        P(head, None),
        P(None, head),
        P(None, head),
        P(None, head),
    )
    out_specs = P("seq", head)
    return jax.shard_map(
        make_body(n_zhi, n_x, n_core),
        mesh=fine,
        in_specs=in_specs,
        out_specs=out_specs,
        check_vma=False,
    )
```

```python
import jax
import jax.numpy as jnp
from jax import lax
from jax.sharding import Mesh
from jax.sharding import PartitionSpec as P

WINDOW = 1024
NBR = 4


score_scale = 168.0 ** (-0.5)


def from_behind(block, axis, distance):
    devices = range(lax.axis_size(axis))
    route = [(i - distance, i) for i in devices if i - distance in devices]
    return lax.ppermute(block, axis, route)


def shift(block, axis, size, step):
    return lax.ppermute(block, axis, [(i, (i + step) % size) for i in range(size)])


def gather_axis(block, axis, size):
    if size == 4:
        return ring_gather(block, axis)
    me = lax.axis_index(axis)
    buf = jnp.zeros((size,) + block.shape, block.dtype)
    buf = lax.dynamic_update_index_in_dim(buf, block, me, 0)
    for step in range(1, size):
        got = shift(block, axis, size, step)
        buf = lax.dynamic_update_index_in_dim(buf, got, (me - step) % size, 0)
    return buf


def ring_gather(block, axis):
    me = lax.axis_index(axis)
    half = block.shape[0] // 2
    ahead = shift(block, axis, 4, 1)
    behind = shift(block, axis, 4, -1)
    far = jnp.concatenate(
        [shift(ahead[:half], axis, 4, 1), shift(behind[half:], axis, 4, -1)], axis=0
    )
    buf = jnp.zeros((4,) + block.shape, block.dtype)
    buf = lax.dynamic_update_index_in_dim(buf, block, me, 0)
    buf = lax.dynamic_update_index_in_dim(buf, ahead, (me + 3) % 4, 0)
    buf = lax.dynamic_update_index_in_dim(buf, behind, (me + 1) % 4, 0)
    return lax.dynamic_update_index_in_dim(buf, far, (me + 2) % 4, 0)


def ring_scatter(parts, axis, dim):
    me = lax.axis_index(axis)

    def piece(k):
        return lax.dynamic_index_in_dim(parts, k % 4, dim, keepdims=False).astype(jnp.float32)

    far = piece(me + 2)
    half = far.shape[0] // 2
    got_a = shift(far[:half].astype(jnp.bfloat16), axis, 4, 1).astype(jnp.float32)
    got_b = shift(far[half:].astype(jnp.bfloat16), axis, 4, -1).astype(jnp.float32)
    up = piece(me + 1)
    up = jnp.concatenate([up[:half] + got_a, up[half:]], axis=0)
    down = piece(me + 3)
    down = jnp.concatenate([down[:half], down[half:] + got_b], axis=0)
    acc = piece(me)
    acc = acc + shift(up.astype(jnp.bfloat16), axis, 4, 1).astype(jnp.float32)
    return acc + shift(down.astype(jnp.bfloat16), axis, 4, -1).astype(jnp.float32)


def scatter_axis(parts, axis, size, dim):
    if size == 4:
        return ring_scatter(parts, axis, dim)
    me = lax.axis_index(axis)
    acc = lax.dynamic_index_in_dim(parts, me, dim, keepdims=False).astype(jnp.float32)
    for step in range(1, size):
        out = lax.dynamic_index_in_dim(parts, (me + step) % size, dim, keepdims=False)
        acc = acc + shift(out.astype(jnp.bfloat16), axis, size, step).astype(jnp.float32)
    return acc


def dot_rows(left, right):
    return lax.dot_general(
        left, right, (((1,), (1,)), ((), ())), preferred_element_type=jnp.float32
    )


def dot_cols(left, right):
    return lax.dot_general(
        left, right, (((0,), (0,)), ((), ())), preferred_element_type=jnp.float32
    )


def band_backward(query_block, key_band, value_band, grad_block, query_start, key_start):
    length = query_block.shape[0]
    span = key_band.shape[0]
    query_pos = query_start + jnp.arange(length, dtype=jnp.int32)
    key_pos = key_start + jnp.arange(span, dtype=jnp.int32)
    offset = query_pos[:, None] - key_pos[None, :]
    allowed = (key_pos[None, :] >= 0) & (offset >= 0) & (offset < WINDOW)
    scores = dot_rows(query_block, key_band) * score_scale
    masked = jnp.where(allowed, scores, -1e30)
    top = jnp.max(masked, axis=1, keepdims=True)
    weights = jnp.where(allowed, jnp.exp(masked - top), 0.0)
    probs = weights / jnp.sum(weights, axis=1, keepdims=True)
    probs_low = probs.astype(jnp.bfloat16)
    grad_probs = dot_rows(grad_block, value_band)
    delta = jnp.sum(probs * grad_probs, axis=1, keepdims=True)
    grad_scores = (probs * (grad_probs - delta)).astype(jnp.bfloat16)
    grad_query = (
        jnp.dot(grad_scores, key_band, preferred_element_type=jnp.float32) * score_scale
    ).astype(jnp.bfloat16)
    grad_keys = (dot_cols(grad_scores, query_block) * score_scale).astype(jnp.bfloat16)
    grad_values = dot_cols(probs_low, grad_block).astype(jnp.bfloat16)
    return (grad_query, grad_keys, grad_values)


def make_body(n_zhi, n_x, n_core):
    def body(query, keys, values, d_out, w_out, w_query, w_key, w_value):
        length, dim = query.shape
        width = d_out.shape[1]
        seq_index = lax.axis_index("seq")
        stacked = gather_axis(d_out, "zhi", n_zhi)
        stacked = gather_axis(stacked, "x", n_x)
        stacked = gather_axis(stacked, "core", n_core)
        out_rows = w_out.reshape(w_out.shape[0], n_zhi, n_x, n_core, width)
        grad_heads = jnp.einsum(
            "cxzti,hzxci->th", stacked, out_rows, preferred_element_type=jnp.float32
        ).astype(jnp.bfloat16)
        reach = NBR
        kv = jnp.concatenate([keys, values], axis=1)
        kv_blocks = [from_behind(kv, "seq", distance) for distance in range(reach, 0, -1)]
        kv_band = jnp.concatenate(kv_blocks + [kv], axis=0)
        key_band = kv_band[:, :dim]
        value_band = kv_band[:, dim:]
        query_start = seq_index * length
        grad_query, key_parts, value_parts = band_backward(
            query, key_band, value_band, grad_heads, query_start, query_start - reach * length
        )
        kv_parts = jnp.concatenate([key_parts, value_parts], axis=1)
        kv_total = kv_parts[reach * length :].astype(jnp.float32)
        for distance in range(1, reach + 1):
            first = (reach - distance) * length
            back = from_behind(kv_parts[first : first + length], "seq", -distance)
            kv_total = kv_total + back.astype(jnp.float32)
        kv_total = kv_total.astype(jnp.bfloat16)
        grad_keys = kv_total[:, :dim]
        grad_values = kv_total[:, dim:]
        summed = dot_rows(w_query, grad_query)
        summed = summed + dot_rows(w_key, grad_keys)
        summed = summed + dot_rows(w_value, grad_values)
        term = summed.astype(jnp.bfloat16).reshape(n_zhi, n_x, n_core, width, length)
        part = scatter_axis(term, "core", n_core, 2)
        part = scatter_axis(part, "x", n_x, 1)
        part = scatter_axis(part, "zhi", n_zhi, 0)
        return part.T.astype(jnp.bfloat16)

    return body


def solution(mesh):
    n_seq, n_head = mesh.devices.shape
    n_core = 2
    n_x = len({d.coords[0] for d in mesh.devices[0]})
    n_zhi = n_head // (n_x * n_core)
    fine = Mesh(mesh.devices.reshape(n_seq, n_zhi, n_x, n_core), ("seq", "zhi", "x", "core"))
    head = ("zhi", "x", "core")
    in_specs = (
        P("seq", head),
        P("seq", head),
        P("seq", head),
        P("seq", head),
        P(head, None),
        P(None, head),
        P(None, head),
        P(None, head),
    )
    out_specs = P("seq", head)
    return jax.shard_map(
        make_body(n_zhi, n_x, n_core),
        mesh=fine,
        in_specs=in_specs,
        out_specs=out_specs,
        check_vma=False,
    )
```

```python
import jax
import jax.numpy as jnp
from jax import lax
from jax.sharding import Mesh
from jax.sharding import PartitionSpec as P

WINDOW = 1024
NBR = 4


score_scale = 168.0 ** (-0.5)


def from_behind(block, axis, distance):
    devices = range(lax.axis_size(axis))
    route = [(i - distance, i) for i in devices if i - distance in devices]
    return lax.ppermute(block, axis, route)


def shift(block, axis, size, step):
    return lax.ppermute(block, axis, [(i, (i + step) % size) for i in range(size)])


def gather_axis(block, axis, size, relay=False):
    if relay and size == 4:
        return ring_gather(block, axis)
    me = lax.axis_index(axis)
    buf = jnp.zeros((size,) + block.shape, block.dtype)
    buf = lax.dynamic_update_index_in_dim(buf, block, me, 0)
    for step in range(1, size):
        got = shift(block, axis, size, step)
        buf = lax.dynamic_update_index_in_dim(buf, got, (me - step) % size, 0)
    return buf


def ring_gather(block, axis):
    me = lax.axis_index(axis)
    ahead = shift(block, axis, 4, 1)
    behind = shift(block, axis, 4, -1)
    far = shift(ahead, axis, 4, 1)
    buf = jnp.zeros((4,) + block.shape, block.dtype)
    buf = lax.dynamic_update_index_in_dim(buf, block, me, 0)
    buf = lax.dynamic_update_index_in_dim(buf, ahead, (me + 3) % 4, 0)
    buf = lax.dynamic_update_index_in_dim(buf, behind, (me + 1) % 4, 0)
    return lax.dynamic_update_index_in_dim(buf, far, (me + 2) % 4, 0)


def ring_scatter(parts, axis, dim):
    me = lax.axis_index(axis)

    def piece(k):
        return lax.dynamic_index_in_dim(parts, k % 4, dim, keepdims=False).astype(jnp.float32)

    got = shift(piece(me + 2).astype(jnp.bfloat16), axis, 4, 1).astype(jnp.float32)
    up = (piece(me + 1) + got).astype(jnp.bfloat16)
    down = piece(me + 3).astype(jnp.bfloat16)
    acc = piece(me)
    acc = acc + shift(up, axis, 4, 1).astype(jnp.float32)
    return acc + shift(down, axis, 4, -1).astype(jnp.float32)


def scatter_axis(parts, axis, size, dim, relay=False):
    if relay and size == 4:
        return ring_scatter(parts, axis, dim)
    me = lax.axis_index(axis)
    acc = lax.dynamic_index_in_dim(parts, me, dim, keepdims=False).astype(jnp.float32)
    for step in range(1, size):
        out = lax.dynamic_index_in_dim(parts, (me + step) % size, dim, keepdims=False)
        acc = acc + shift(out.astype(jnp.bfloat16), axis, size, step).astype(jnp.float32)
    return acc


def dot_rows(left, right):
    return lax.dot_general(
        left, right, (((1,), (1,)), ((), ())), preferred_element_type=jnp.float32
    )


def dot_cols(left, right):
    return lax.dot_general(
        left, right, (((0,), (0,)), ((), ())), preferred_element_type=jnp.float32
    )


def band_backward(query_block, key_band, value_band, grad_block, query_start, key_start):
    length = query_block.shape[0]
    span = key_band.shape[0]
    query_pos = query_start + jnp.arange(length, dtype=jnp.int32)
    key_pos = key_start + jnp.arange(span, dtype=jnp.int32)
    offset = query_pos[:, None] - key_pos[None, :]
    allowed = (key_pos[None, :] >= 0) & (offset >= 0) & (offset < WINDOW)
    scores = dot_rows(query_block, key_band) * score_scale
    masked = jnp.where(allowed, scores, -1e30)
    top = jnp.max(masked, axis=1, keepdims=True)
    weights = jnp.where(allowed, jnp.exp(masked - top), 0.0)
    probs = weights / jnp.sum(weights, axis=1, keepdims=True)
    probs_low = probs.astype(jnp.bfloat16)
    grad_probs = dot_rows(grad_block, value_band)
    delta = jnp.sum(probs * grad_probs, axis=1, keepdims=True)
    grad_scores = (probs * (grad_probs - delta)).astype(jnp.bfloat16)
    grad_query = (
        jnp.dot(grad_scores, key_band, preferred_element_type=jnp.float32) * score_scale
    ).astype(jnp.bfloat16)
    grad_keys = (dot_cols(grad_scores, query_block) * score_scale).astype(jnp.bfloat16)
    grad_values = dot_cols(probs_low, grad_block).astype(jnp.bfloat16)
    return (grad_query, grad_keys, grad_values)


def make_body(n_zhi, n_x, n_core):
    def body(query, keys, values, d_out, w_out, w_query, w_key, w_value):
        length, dim = query.shape
        width = d_out.shape[1]
        seq_index = lax.axis_index("seq")
        stacked = gather_axis(d_out, "zhi", n_zhi, relay=True)
        stacked = gather_axis(stacked, "x", n_x)
        stacked = gather_axis(stacked, "core", n_core)
        out_rows = w_out.reshape(w_out.shape[0], n_zhi, n_x, n_core, width)
        grad_heads = jnp.einsum(
            "cxzti,hzxci->th", stacked, out_rows, preferred_element_type=jnp.float32
        ).astype(jnp.bfloat16)
        reach = NBR
        kv = jnp.concatenate([keys, values], axis=1)
        kv_blocks = [from_behind(kv, "seq", distance) for distance in range(reach, 0, -1)]
        kv_band = jnp.concatenate(kv_blocks + [kv], axis=0)
        key_band = kv_band[:, :dim]
        value_band = kv_band[:, dim:]
        query_start = seq_index * length
        grad_query, key_parts, value_parts = band_backward(
            query, key_band, value_band, grad_heads, query_start, query_start - reach * length
        )
        kv_parts = jnp.concatenate([key_parts, value_parts], axis=1)
        kv_total = kv_parts[reach * length :].astype(jnp.float32)
        for distance in range(1, reach + 1):
            first = (reach - distance) * length
            back = from_behind(kv_parts[first : first + length], "seq", -distance)
            kv_total = kv_total + back.astype(jnp.float32)
        kv_total = kv_total.astype(jnp.bfloat16)
        grad_keys = kv_total[:, :dim]
        grad_values = kv_total[:, dim:]
        summed = dot_rows(w_query, grad_query)
        summed = summed + dot_rows(w_key, grad_keys)
        summed = summed + dot_rows(w_value, grad_values)
        term = summed.astype(jnp.bfloat16).reshape(n_zhi, n_x, n_core, width, length)
        part = scatter_axis(term, "core", n_core, 2)
        part = scatter_axis(part, "x", n_x, 1)
        part = scatter_axis(part, "zhi", n_zhi, 0, relay=True)
        return part.T.astype(jnp.bfloat16)

    return body


def solution(mesh):
    n_seq, n_head = mesh.devices.shape
    n_core = 2
    n_x = len({d.coords[0] for d in mesh.devices[0]})
    n_zhi = n_head // (n_x * n_core)
    fine = Mesh(mesh.devices.reshape(n_seq, n_zhi, n_x, n_core), ("seq", "zhi", "x", "core"))
    head = ("zhi", "x", "core")
    in_specs = (
        P("seq", head),
        P("seq", head),
        P("seq", head),
        P("seq", head),
        P(head, None),
        P(None, head),
        P(None, head),
        P(None, head),
    )
    out_specs = P("seq", head)
    return jax.shard_map(
        make_body(n_zhi, n_x, n_core),
        mesh=fine,
        in_specs=in_specs,
        out_specs=out_specs,
        check_vma=False,
    )
```

```python
import jax
import jax.numpy as jnp
from jax import lax
from jax.sharding import Mesh
from jax.sharding import PartitionSpec as P

WINDOW = 1024
NBR = 4


score_scale = 168.0 ** (-0.5)


def from_behind(block, axis, distance):
    devices = range(lax.axis_size(axis))
    route = [(i - distance, i) for i in devices if i - distance in devices]
    return lax.ppermute(block, axis, route)


def shift(block, axis, size, step):
    return lax.ppermute(block, axis, [(i, (i + step) % size) for i in range(size)])


def gather_axis(block, axis, size, relay=False):
    if relay and size == 4:
        return ring_gather(block, axis)
    me = lax.axis_index(axis)
    buf = jnp.zeros((size,) + block.shape, block.dtype)
    buf = lax.dynamic_update_index_in_dim(buf, block, me, 0)
    for step in range(1, size):
        got = shift(block, axis, size, step)
        buf = lax.dynamic_update_index_in_dim(buf, got, (me - step) % size, 0)
    return buf


def ring_gather(block, axis):
    me = lax.axis_index(axis)
    ahead = shift(block, axis, 4, 1)
    behind = shift(block, axis, 4, -1)
    far = shift(ahead, axis, 4, 1)
    buf = jnp.zeros((4,) + block.shape, block.dtype)
    buf = lax.dynamic_update_index_in_dim(buf, block, me, 0)
    buf = lax.dynamic_update_index_in_dim(buf, ahead, (me + 3) % 4, 0)
    buf = lax.dynamic_update_index_in_dim(buf, behind, (me + 1) % 4, 0)
    return lax.dynamic_update_index_in_dim(buf, far, (me + 2) % 4, 0)


def ring_scatter(parts, axis, dim):
    me = lax.axis_index(axis)

    def piece(k):
        return lax.dynamic_index_in_dim(parts, k % 4, dim, keepdims=False).astype(jnp.float32)

    got = shift(piece(me + 2).astype(jnp.bfloat16), axis, 4, 1).astype(jnp.float32)
    up = (piece(me + 1) + got).astype(jnp.bfloat16)
    down = piece(me + 3).astype(jnp.bfloat16)
    acc = piece(me)
    acc = acc + shift(up, axis, 4, 1).astype(jnp.float32)
    return acc + shift(down, axis, 4, -1).astype(jnp.float32)


def scatter_axis(parts, axis, size, dim, relay=False):
    if relay and size == 4:
        return ring_scatter(parts, axis, dim)
    me = lax.axis_index(axis)
    acc = lax.dynamic_index_in_dim(parts, me, dim, keepdims=False).astype(jnp.float32)
    for step in range(1, size):
        out = lax.dynamic_index_in_dim(parts, (me + step) % size, dim, keepdims=False)
        acc = acc + shift(out.astype(jnp.bfloat16), axis, size, step).astype(jnp.float32)
    return acc


def dot_rows(left, right):
    return lax.dot_general(
        left, right, (((1,), (1,)), ((), ())), preferred_element_type=jnp.float32
    )


def dot_cols(left, right):
    return lax.dot_general(
        left, right, (((0,), (0,)), ((), ())), preferred_element_type=jnp.float32
    )


def band_backward(query_block, key_band, value_band, grad_block, query_start, key_start):
    length = query_block.shape[0]
    span = key_band.shape[0]
    query_pos = query_start + jnp.arange(length, dtype=jnp.int32)
    key_pos = key_start + jnp.arange(span, dtype=jnp.int32)
    offset = query_pos[:, None] - key_pos[None, :]
    allowed = (key_pos[None, :] >= 0) & (offset >= 0) & (offset < WINDOW)
    scores = dot_rows(query_block, key_band) * score_scale
    masked = jnp.where(allowed, scores, -1e30)
    top = jnp.max(masked, axis=1, keepdims=True)
    weights = jnp.where(allowed, jnp.exp(masked - top), 0.0)
    probs = weights / jnp.sum(weights, axis=1, keepdims=True)
    probs_low = probs.astype(jnp.bfloat16)
    grad_probs = dot_rows(grad_block, value_band)
    delta = jnp.sum(probs * grad_probs, axis=1, keepdims=True)
    grad_scores = (probs * (grad_probs - delta)).astype(jnp.bfloat16)
    grad_query = (
        jnp.dot(grad_scores, key_band, preferred_element_type=jnp.float32) * score_scale
    ).astype(jnp.bfloat16)
    grad_keys = (dot_cols(grad_scores, query_block) * score_scale).astype(jnp.bfloat16)
    grad_values = dot_cols(probs_low, grad_block).astype(jnp.bfloat16)
    return (grad_query, grad_keys, grad_values)


def make_body(n_zhi, n_x, n_core):
    def body(query, keys, values, d_out, w_out, w_query, w_key, w_value):
        length, dim = query.shape
        width = d_out.shape[1]
        seq_index = lax.axis_index("seq")
        stacked = gather_axis(d_out, "zhi", n_zhi, relay=True)
        stacked = gather_axis(stacked, "x", n_x, relay=True)
        stacked = gather_axis(stacked, "core", n_core)
        out_rows = w_out.reshape(w_out.shape[0], n_zhi, n_x, n_core, width)
        grad_heads = jnp.einsum(
            "cxzti,hzxci->th", stacked, out_rows, preferred_element_type=jnp.float32
        ).astype(jnp.bfloat16)
        reach = NBR
        kv = jnp.concatenate([keys, values], axis=1)
        kv_blocks = [from_behind(kv, "seq", distance) for distance in range(reach, 0, -1)]
        kv_band = jnp.concatenate(kv_blocks + [kv], axis=0)
        key_band = kv_band[:, :dim]
        value_band = kv_band[:, dim:]
        query_start = seq_index * length
        grad_query, key_parts, value_parts = band_backward(
            query, key_band, value_band, grad_heads, query_start, query_start - reach * length
        )
        kv_parts = jnp.concatenate([key_parts, value_parts], axis=1)
        kv_total = kv_parts[reach * length :].astype(jnp.float32)
        for distance in range(1, reach + 1):
            first = (reach - distance) * length
            back = from_behind(kv_parts[first : first + length], "seq", -distance)
            kv_total = kv_total + back.astype(jnp.float32)
        kv_total = kv_total.astype(jnp.bfloat16)
        grad_keys = kv_total[:, :dim]
        grad_values = kv_total[:, dim:]
        summed = dot_rows(w_query, grad_query)
        summed = summed + dot_rows(w_key, grad_keys)
        summed = summed + dot_rows(w_value, grad_values)
        term = summed.astype(jnp.bfloat16).reshape(n_zhi, n_x, n_core, width, length)
        part = scatter_axis(term, "core", n_core, 2)
        part = scatter_axis(part, "x", n_x, 1, relay=True)
        part = scatter_axis(part, "zhi", n_zhi, 0, relay=True)
        return part.T.astype(jnp.bfloat16)

    return body


def solution(mesh):
    n_seq, n_head = mesh.devices.shape
    n_core = 2
    n_x = len({d.coords[0] for d in mesh.devices[0]})
    n_zhi = n_head // (n_x * n_core)
    fine = Mesh(mesh.devices.reshape(n_seq, n_zhi, n_x, n_core), ("seq", "zhi", "x", "core"))
    head = ("zhi", "x", "core")
    in_specs = (
        P("seq", head),
        P("seq", head),
        P("seq", head),
        P("seq", head),
        P(head, None),
        P(None, head),
        P(None, head),
        P(None, head),
    )
    out_specs = P("seq", head)
    return jax.shard_map(
        make_body(n_zhi, n_x, n_core),
        mesh=fine,
        in_specs=in_specs,
        out_specs=out_specs,
        check_vma=False,
    )
```

```python
import jax
import jax.numpy as jnp
from jax import lax
from jax.sharding import Mesh
from jax.sharding import PartitionSpec as P

WINDOW = 1024
NBR = 4


score_scale = 168.0 ** (-0.5)


def from_behind(block, axis, distance):
    devices = range(lax.axis_size(axis))
    route = [(i - distance, i) for i in devices if i - distance in devices]
    return lax.ppermute(block, axis, route)


def shift(block, axis, size, step):
    return lax.ppermute(block, axis, [(i, (i + step) % size) for i in range(size)])


def gather_axis(block, axis, size, relay=False):
    if relay and size == 4:
        return ring_gather(block, axis)
    me = lax.axis_index(axis)
    buf = jnp.zeros((size,) + block.shape, block.dtype)
    buf = lax.dynamic_update_index_in_dim(buf, block, me, 0)
    for step in range(1, size):
        got = shift(block, axis, size, step)
        buf = lax.dynamic_update_index_in_dim(buf, got, (me - step) % size, 0)
    return buf


def ring_gather(block, axis):
    me = lax.axis_index(axis)
    ahead = shift(block, axis, 4, 1)
    behind = shift(block, axis, 4, -1)
    far = shift(ahead, axis, 4, 1)
    buf = jnp.zeros((4,) + block.shape, block.dtype)
    buf = lax.dynamic_update_index_in_dim(buf, block, me, 0)
    buf = lax.dynamic_update_index_in_dim(buf, ahead, (me + 3) % 4, 0)
    buf = lax.dynamic_update_index_in_dim(buf, behind, (me + 1) % 4, 0)
    return lax.dynamic_update_index_in_dim(buf, far, (me + 2) % 4, 0)


def ring_scatter(parts, axis, dim):
    me = lax.axis_index(axis)

    def piece(k):
        return lax.dynamic_index_in_dim(parts, k % 4, dim, keepdims=False).astype(jnp.float32)

    got = shift(piece(me + 2).astype(jnp.bfloat16), axis, 4, 1).astype(jnp.float32)
    up = (piece(me + 1) + got).astype(jnp.bfloat16)
    down = piece(me + 3).astype(jnp.bfloat16)
    acc = piece(me)
    acc = acc + shift(up, axis, 4, 1).astype(jnp.float32)
    return acc + shift(down, axis, 4, -1).astype(jnp.float32)


def scatter_axis(parts, axis, size, dim, relay=False):
    if relay and size == 4:
        return ring_scatter(parts, axis, dim)
    me = lax.axis_index(axis)
    acc = lax.dynamic_index_in_dim(parts, me, dim, keepdims=False).astype(jnp.float32)
    for step in range(1, size):
        out = lax.dynamic_index_in_dim(parts, (me + step) % size, dim, keepdims=False)
        acc = acc + shift(out.astype(jnp.bfloat16), axis, size, step).astype(jnp.float32)
    return acc


def dot_rows(left, right):
    return lax.dot_general(
        left, right, (((1,), (1,)), ((), ())), preferred_element_type=jnp.float32
    )


def dot_cols(left, right):
    return lax.dot_general(
        left, right, (((0,), (0,)), ((), ())), preferred_element_type=jnp.float32
    )


def band_backward(query_block, key_band, value_band, grad_block, query_start, key_start):
    length = query_block.shape[0]
    span = key_band.shape[0]
    query_pos = query_start + jnp.arange(length, dtype=jnp.int32)
    key_pos = key_start + jnp.arange(span, dtype=jnp.int32)
    offset = query_pos[:, None] - key_pos[None, :]
    allowed = (key_pos[None, :] >= 0) & (offset >= 0) & (offset < WINDOW)
    scores = dot_rows(query_block, key_band) * score_scale
    masked = jnp.where(allowed, scores, -1e30)
    top = jnp.max(masked, axis=1, keepdims=True)
    weights = jnp.where(allowed, jnp.exp(masked - top), 0.0)
    probs = weights / jnp.sum(weights, axis=1, keepdims=True)
    probs_low = probs.astype(jnp.bfloat16)
    grad_probs = dot_rows(grad_block, value_band)
    delta = jnp.sum(probs * grad_probs, axis=1, keepdims=True)
    grad_scores = (probs * (grad_probs - delta)).astype(jnp.bfloat16)
    grad_query = (
        jnp.dot(grad_scores, key_band, preferred_element_type=jnp.float32) * score_scale
    ).astype(jnp.bfloat16)
    grad_keys = (dot_cols(grad_scores, query_block) * score_scale).astype(jnp.bfloat16)
    grad_values = dot_cols(probs_low, grad_block).astype(jnp.bfloat16)
    return (grad_query, grad_keys, grad_values)


def make_body(n_zhi, n_x, n_core):
    def body(query, keys, values, d_out, w_out, w_query, w_key, w_value):
        length, dim = query.shape
        width = d_out.shape[1]
        seq_index = lax.axis_index("seq")
        stacked = gather_axis(d_out, "zhi", n_zhi, relay=True)
        stacked = gather_axis(stacked, "x", n_x)
        stacked = gather_axis(stacked, "core", n_core)
        out_rows = w_out.reshape(w_out.shape[0], n_zhi, n_x, n_core, width)
        grad_heads = jnp.einsum(
            "cxzti,hzxci->th", stacked, out_rows, preferred_element_type=jnp.float32
        ).astype(jnp.bfloat16)
        reach = NBR
        kv = jnp.concatenate([keys, values], axis=1)
        kv_blocks = [from_behind(kv, "seq", distance) for distance in range(reach, 0, -1)]
        kv_band = jnp.concatenate(kv_blocks + [kv], axis=0)
        key_band = kv_band[:, :dim]
        value_band = kv_band[:, dim:]
        query_start = seq_index * length
        grad_query, key_parts, value_parts = band_backward(
            query, key_band, value_band, grad_heads, query_start, query_start - reach * length
        )
        kv_parts = jnp.concatenate([key_parts, value_parts], axis=1)
        kv_total = kv_parts[reach * length :].astype(jnp.float32)
        for distance in range(1, reach + 1):
            first = (reach - distance) * length
            back = from_behind(kv_parts[first : first + length], "seq", -distance)
            kv_total = kv_total + back.astype(jnp.float32)
        kv_total = kv_total.astype(jnp.bfloat16)
        grad_keys = kv_total[:, :dim]
        grad_values = kv_total[:, dim:]
        core_index = lax.axis_index("core")

        def project(index):
            def rows(w):
                w = w.reshape(n_zhi, n_x, n_core, width, dim)
                return lax.dynamic_index_in_dim(w, index, 2, keepdims=False).reshape(-1, dim)

            summed = dot_rows(rows(w_query), grad_query)
            summed = summed + dot_rows(rows(w_key), grad_keys)
            summed = summed + dot_rows(rows(w_value), grad_values)
            return summed.astype(jnp.bfloat16).reshape(n_zhi, n_x, width, length)

        keep = project(core_index)
        sent = shift(project((core_index + 1) % n_core), "core", n_core, 1)
        part = keep.astype(jnp.float32) + sent.astype(jnp.float32)
        part = scatter_axis(part, "x", n_x, 1)
        part = scatter_axis(part, "zhi", n_zhi, 0, relay=True)
        return part.T.astype(jnp.bfloat16)

    return body


def solution(mesh):
    n_seq, n_head = mesh.devices.shape
    n_core = 2
    n_x = len({d.coords[0] for d in mesh.devices[0]})
    n_zhi = n_head // (n_x * n_core)
    fine = Mesh(mesh.devices.reshape(n_seq, n_zhi, n_x, n_core), ("seq", "zhi", "x", "core"))
    head = ("zhi", "x", "core")
    in_specs = (
        P("seq", head),
        P("seq", head),
        P("seq", head),
        P("seq", head),
        P(head, None),
        P(None, head),
        P(None, head),
        P(None, head),
    )
    out_specs = P("seq", head)
    return jax.shard_map(
        make_body(n_zhi, n_x, n_core),
        mesh=fine,
        in_specs=in_specs,
        out_specs=out_specs,
        check_vma=False,
    )
```

```python
import jax
import jax.numpy as jnp
from jax import lax
from jax.sharding import Mesh
from jax.sharding import PartitionSpec as P

WINDOW = 1024
NBR = 4


score_scale = 168.0 ** (-0.5)


def from_behind(block, axis, distance):
    devices = range(lax.axis_size(axis))
    route = [(i - distance, i) for i in devices if i - distance in devices]
    return lax.ppermute(block, axis, route)


def shift(block, axis, size, step):
    return lax.ppermute(block, axis, [(i, (i + step) % size) for i in range(size)])


def gather_axis(block, axis, size, relay=False):
    if relay and size == 4:
        return ring_gather(block, axis)
    me = lax.axis_index(axis)
    buf = jnp.zeros((size,) + block.shape, block.dtype)
    buf = lax.dynamic_update_index_in_dim(buf, block, me, 0)
    for step in range(1, size):
        got = shift(block, axis, size, step)
        buf = lax.dynamic_update_index_in_dim(buf, got, (me - step) % size, 0)
    return buf


def ring_gather(block, axis):
    me = lax.axis_index(axis)
    ahead = shift(block, axis, 4, 1)
    behind = shift(block, axis, 4, -1)
    far = shift(ahead, axis, 4, 1)
    buf = jnp.zeros((4,) + block.shape, block.dtype)
    buf = lax.dynamic_update_index_in_dim(buf, block, me, 0)
    buf = lax.dynamic_update_index_in_dim(buf, ahead, (me + 3) % 4, 0)
    buf = lax.dynamic_update_index_in_dim(buf, behind, (me + 1) % 4, 0)
    return lax.dynamic_update_index_in_dim(buf, far, (me + 2) % 4, 0)


def ring_scatter(parts, axis, dim):
    me = lax.axis_index(axis)

    def piece(k):
        return lax.dynamic_index_in_dim(parts, k % 4, dim, keepdims=False).astype(jnp.float32)

    got = shift(piece(me + 2).astype(jnp.bfloat16), axis, 4, 1).astype(jnp.float32)
    up = (piece(me + 1) + got).astype(jnp.bfloat16)
    down = piece(me + 3).astype(jnp.bfloat16)
    acc = piece(me)
    acc = acc + shift(up, axis, 4, 1).astype(jnp.float32)
    return acc + shift(down, axis, 4, -1).astype(jnp.float32)


def scatter_axis(parts, axis, size, dim, relay=False):
    if relay and size == 4:
        return ring_scatter(parts, axis, dim)
    me = lax.axis_index(axis)
    acc = lax.dynamic_index_in_dim(parts, me, dim, keepdims=False).astype(jnp.float32)
    for step in range(1, size):
        out = lax.dynamic_index_in_dim(parts, (me + step) % size, dim, keepdims=False)
        acc = acc + shift(out.astype(jnp.bfloat16), axis, size, step).astype(jnp.float32)
    return acc


def dot_rows(left, right):
    return lax.dot_general(
        left, right, (((1,), (1,)), ((), ())), preferred_element_type=jnp.float32
    )


def dot_cols(left, right):
    return lax.dot_general(
        left, right, (((0,), (0,)), ((), ())), preferred_element_type=jnp.float32
    )


def band_backward(query_block, key_band, value_band, grad_block, query_start, key_start):
    length = query_block.shape[0]
    span = key_band.shape[0]
    query_pos = query_start + jnp.arange(length, dtype=jnp.int32)
    key_pos = key_start + jnp.arange(span, dtype=jnp.int32)
    offset = query_pos[:, None] - key_pos[None, :]
    allowed = (key_pos[None, :] >= 0) & (offset >= 0) & (offset < WINDOW)
    scores = dot_rows(query_block, key_band) * score_scale
    masked = jnp.where(allowed, scores, -1e30)
    top = jnp.max(masked, axis=1, keepdims=True)
    weights = jnp.where(allowed, jnp.exp(masked - top), 0.0)
    probs = weights / jnp.sum(weights, axis=1, keepdims=True)
    probs_low = probs.astype(jnp.bfloat16)
    grad_probs = dot_rows(grad_block, value_band)
    delta = jnp.sum(probs * grad_probs, axis=1, keepdims=True)
    grad_scores = (probs * (grad_probs - delta)).astype(jnp.bfloat16)
    grad_query = (
        jnp.dot(grad_scores, key_band, preferred_element_type=jnp.float32) * score_scale
    ).astype(jnp.bfloat16)
    grad_keys = (dot_cols(grad_scores, query_block) * score_scale).astype(jnp.bfloat16)
    grad_values = dot_cols(probs_low, grad_block).astype(jnp.bfloat16)
    return (grad_query, grad_keys, grad_values)


def make_body(n_zhi, n_x, n_core):
    def body(query, keys, values, d_out, w_out, w_query, w_key, w_value):
        length, dim = query.shape
        width = d_out.shape[1]
        seq_index = lax.axis_index("seq")
        stacked = gather_axis(d_out, "zhi", n_zhi, relay=True)
        kv = jnp.concatenate([keys, values], axis=1)
        stacked, kv = lax.optimization_barrier((stacked, kv))
        stacked = gather_axis(stacked, "x", n_x)
        stacked = gather_axis(stacked, "core", n_core)
        out_rows = w_out.reshape(w_out.shape[0], n_zhi, n_x, n_core, width)
        grad_heads = jnp.einsum(
            "cxzti,hzxci->th", stacked, out_rows, preferred_element_type=jnp.float32
        ).astype(jnp.bfloat16)
        reach = NBR
        kv_blocks = [from_behind(kv, "seq", distance) for distance in range(reach, 0, -1)]
        kv_band = jnp.concatenate(kv_blocks + [kv], axis=0)
        key_band = kv_band[:, :dim]
        value_band = kv_band[:, dim:]
        query_start = seq_index * length
        grad_query, key_parts, value_parts = band_backward(
            query, key_band, value_band, grad_heads, query_start, query_start - reach * length
        )
        kv_parts = jnp.concatenate([key_parts, value_parts], axis=1)
        kv_total = kv_parts[reach * length :].astype(jnp.float32)
        for distance in range(1, reach + 1):
            first = (reach - distance) * length
            back = from_behind(kv_parts[first : first + length], "seq", -distance)
            kv_total = kv_total + back.astype(jnp.float32)
        kv_total = kv_total.astype(jnp.bfloat16)
        grad_keys = kv_total[:, :dim]
        grad_values = kv_total[:, dim:]
        core_index = lax.axis_index("core")

        def project(index):
            def rows(w):
                w = w.reshape(n_zhi, n_x, n_core, width, dim)
                return lax.dynamic_index_in_dim(w, index, 2, keepdims=False).reshape(-1, dim)

            summed = dot_rows(rows(w_query), grad_query)
            summed = summed + dot_rows(rows(w_key), grad_keys)
            summed = summed + dot_rows(rows(w_value), grad_values)
            return summed.astype(jnp.bfloat16).reshape(n_zhi, n_x, width, length)

        keep = project(core_index)
        sent = shift(project((core_index + 1) % n_core), "core", n_core, 1)
        part = keep.astype(jnp.float32) + sent.astype(jnp.float32)
        part = scatter_axis(part, "x", n_x, 1)
        part = scatter_axis(part, "zhi", n_zhi, 0, relay=True)
        return part.T.astype(jnp.bfloat16)

    return body


def solution(mesh):
    n_seq, n_head = mesh.devices.shape
    n_core = 2
    n_x = len({d.coords[0] for d in mesh.devices[0]})
    n_zhi = n_head // (n_x * n_core)
    fine = Mesh(mesh.devices.reshape(n_seq, n_zhi, n_x, n_core), ("seq", "zhi", "x", "core"))
    head = ("zhi", "x", "core")
    in_specs = (
        P("seq", head),
        P("seq", head),
        P("seq", head),
        P("seq", head),
        P(head, None),
        P(None, head),
        P(None, head),
        P(None, head),
    )
    out_specs = P("seq", head)
    return jax.shard_map(
        make_body(n_zhi, n_x, n_core),
        mesh=fine,
        in_specs=in_specs,
        out_specs=out_specs,
        check_vma=False,
    )
```

```python
import jax
import jax.numpy as jnp
from jax import lax
from jax.sharding import Mesh
from jax.sharding import PartitionSpec as P

WINDOW = 1024
NBR = 4


score_scale = 168.0 ** (-0.5)


def from_behind(block, axis, distance):
    devices = range(lax.axis_size(axis))
    route = [(i - distance, i) for i in devices if i - distance in devices]
    return lax.ppermute(block, axis, route)


def shift(block, axis, size, step):
    return lax.ppermute(block, axis, [(i, (i + step) % size) for i in range(size)])


def gather_axis(block, axis, size, relay=False):
    if relay and size == 4:
        return ring_gather(block, axis)
    me = lax.axis_index(axis)
    buf = jnp.zeros((size,) + block.shape, block.dtype)
    buf = lax.dynamic_update_index_in_dim(buf, block, me, 0)
    for step in range(1, size):
        got = shift(block, axis, size, step)
        buf = lax.dynamic_update_index_in_dim(buf, got, (me - step) % size, 0)
    return buf


def ring_gather(block, axis):
    me = lax.axis_index(axis)
    ahead = shift(block, axis, 4, 1)
    behind = shift(block, axis, 4, -1)
    far = shift(ahead, axis, 4, 1)
    buf = jnp.zeros((4,) + block.shape, block.dtype)
    buf = lax.dynamic_update_index_in_dim(buf, block, me, 0)
    buf = lax.dynamic_update_index_in_dim(buf, ahead, (me + 3) % 4, 0)
    buf = lax.dynamic_update_index_in_dim(buf, behind, (me + 1) % 4, 0)
    return lax.dynamic_update_index_in_dim(buf, far, (me + 2) % 4, 0)


def ring_scatter(parts, axis, dim):
    me = lax.axis_index(axis)

    def piece(k):
        return lax.dynamic_index_in_dim(parts, k % 4, dim, keepdims=False).astype(jnp.float32)

    got = shift(piece(me + 2).astype(jnp.bfloat16), axis, 4, 1).astype(jnp.float32)
    up = (piece(me + 1) + got).astype(jnp.bfloat16)
    down = piece(me + 3).astype(jnp.bfloat16)
    acc = piece(me)
    acc = acc + shift(up, axis, 4, 1).astype(jnp.float32)
    return acc + shift(down, axis, 4, -1).astype(jnp.float32)


def scatter_axis(parts, axis, size, dim, relay=False):
    if relay and size == 4:
        return ring_scatter(parts, axis, dim)
    me = lax.axis_index(axis)
    acc = lax.dynamic_index_in_dim(parts, me, dim, keepdims=False).astype(jnp.float32)
    for step in range(1, size):
        out = lax.dynamic_index_in_dim(parts, (me + step) % size, dim, keepdims=False)
        acc = acc + shift(out.astype(jnp.bfloat16), axis, size, step).astype(jnp.float32)
    return acc


def dot_rows(left, right):
    return lax.dot_general(
        left, right, (((1,), (1,)), ((), ())), preferred_element_type=jnp.float32
    )


def dot_cols(left, right):
    return lax.dot_general(
        left, right, (((0,), (0,)), ((), ())), preferred_element_type=jnp.float32
    )


def band_backward(query_block, key_band, value_band, grad_block, query_start, key_start):
    length = query_block.shape[0]
    span = key_band.shape[0]
    query_pos = query_start + jnp.arange(length, dtype=jnp.int32)
    key_pos = key_start + jnp.arange(span, dtype=jnp.int32)
    offset = query_pos[:, None] - key_pos[None, :]
    allowed = (key_pos[None, :] >= 0) & (offset >= 0) & (offset < WINDOW)
    scores = dot_rows(query_block, key_band) * score_scale
    masked = jnp.where(allowed, scores, -1e30)
    top = jnp.max(masked, axis=1, keepdims=True)
    weights = jnp.where(allowed, jnp.exp(masked - top), 0.0)
    probs = weights / jnp.sum(weights, axis=1, keepdims=True)
    probs_low = probs.astype(jnp.bfloat16)
    grad_probs = dot_rows(grad_block, value_band)
    delta = jnp.sum(probs * grad_probs, axis=1, keepdims=True)
    grad_scores = (probs * (grad_probs - delta)).astype(jnp.bfloat16)
    grad_query = (
        jnp.dot(grad_scores, key_band, preferred_element_type=jnp.float32) * score_scale
    ).astype(jnp.bfloat16)
    grad_keys = (dot_cols(grad_scores, query_block) * score_scale).astype(jnp.bfloat16)
    grad_values = dot_cols(probs_low, grad_block).astype(jnp.bfloat16)
    return (grad_query, grad_keys, grad_values)


def make_body(n_zhi, n_x, n_core):
    def body(query, keys, values, d_out, w_out, w_query, w_key, w_value):
        length, dim = query.shape
        width = d_out.shape[1]
        seq_index = lax.axis_index("seq")
        stacked = gather_axis(d_out, "zhi", n_zhi, relay=True)
        stacked = gather_axis(stacked, "x", n_x)
        stacked = gather_axis(stacked, "core", n_core)
        out_rows = w_out.reshape(w_out.shape[0], n_zhi, n_x, n_core, width)
        grad_heads = jnp.einsum(
            "cxzti,hzxci->th", stacked, out_rows, preferred_element_type=jnp.float32
        ).astype(jnp.bfloat16)
        reach = NBR
        kv = jnp.concatenate([keys, values], axis=1)
        kv_blocks = [from_behind(kv, "seq", distance) for distance in range(reach, 0, -1)]
        kv_band = jnp.concatenate(kv_blocks + [kv], axis=0)
        key_band = kv_band[:, :dim]
        value_band = kv_band[:, dim:]
        query_start = seq_index * length
        grad_query, key_parts, value_parts = band_backward(
            query, key_band, value_band, grad_heads, query_start, query_start - reach * length
        )
        kv_parts = jnp.concatenate([key_parts, value_parts], axis=1)
        own = kv_parts[reach * length :]
        came = None
        for distance in range(1, reach + 1):
            first = (reach - distance) * length
            back = from_behind(kv_parts[first : first + length], "seq", -distance)
            back = back.astype(jnp.float32)
            came = back if came is None else came + back
        came = came.astype(jnp.bfloat16)
        core_index = lax.axis_index("core")

        def project(index):
            def rows(w):
                w = w.reshape(n_zhi, n_x, n_core, width, dim)
                return lax.dynamic_index_in_dim(w, index, 2, keepdims=False).reshape(-1, dim)

            summed = dot_rows(rows(w_query), grad_query)
            summed = summed + dot_rows(rows(w_key), own[:, :dim])
            summed = summed + dot_rows(rows(w_value), own[:, dim:])
            summed = summed + dot_rows(rows(w_key), came[:, :dim])
            summed = summed + dot_rows(rows(w_value), came[:, dim:])
            return summed.astype(jnp.bfloat16).reshape(n_zhi, n_x, width, length)

        keep = project(core_index)
        sent = shift(project((core_index + 1) % n_core), "core", n_core, 1)
        part = keep.astype(jnp.float32) + sent.astype(jnp.float32)
        part = scatter_axis(part, "x", n_x, 1)
        part = scatter_axis(part, "zhi", n_zhi, 0, relay=True)
        return part.T.astype(jnp.bfloat16)

    return body


def solution(mesh):
    n_seq, n_head = mesh.devices.shape
    n_core = 2
    n_x = len({d.coords[0] for d in mesh.devices[0]})
    n_zhi = n_head // (n_x * n_core)
    fine = Mesh(mesh.devices.reshape(n_seq, n_zhi, n_x, n_core), ("seq", "zhi", "x", "core"))
    head = ("zhi", "x", "core")
    in_specs = (
        P("seq", head),
        P("seq", head),
        P("seq", head),
        P("seq", head),
        P(head, None),
        P(None, head),
        P(None, head),
        P(None, head),
    )
    out_specs = P("seq", head)
    return jax.shard_map(
        make_body(n_zhi, n_x, n_core),
        mesh=fine,
        in_specs=in_specs,
        out_specs=out_specs,
        check_vma=False,
    )
```

```python
import jax
import jax.numpy as jnp
from jax import lax
from jax.sharding import Mesh
from jax.sharding import PartitionSpec as P

WINDOW = 1024
NBR = 4


score_scale = 168.0 ** (-0.5)


def from_behind(block, axis, distance):
    devices = range(lax.axis_size(axis))
    route = [(i - distance, i) for i in devices if i - distance in devices]
    return lax.ppermute(block, axis, route)


def shift(block, axis, size, step):
    return lax.ppermute(block, axis, [(i, (i + step) % size) for i in range(size)])


def gather_axis(block, axis, size, relay=False):
    if relay and size == 4:
        return ring_gather(block, axis)
    me = lax.axis_index(axis)
    buf = jnp.zeros((size,) + block.shape, block.dtype)
    buf = lax.dynamic_update_index_in_dim(buf, block, me, 0)
    for step in range(1, size):
        got = shift(block, axis, size, step)
        buf = lax.dynamic_update_index_in_dim(buf, got, (me - step) % size, 0)
    return buf


def ring_gather(block, axis):
    me = lax.axis_index(axis)
    ahead = shift(block, axis, 4, 1)
    behind = shift(block, axis, 4, -1)
    far = shift(ahead, axis, 4, 1)
    buf = jnp.zeros((4,) + block.shape, block.dtype)
    buf = lax.dynamic_update_index_in_dim(buf, block, me, 0)
    buf = lax.dynamic_update_index_in_dim(buf, ahead, (me + 3) % 4, 0)
    buf = lax.dynamic_update_index_in_dim(buf, behind, (me + 1) % 4, 0)
    return lax.dynamic_update_index_in_dim(buf, far, (me + 2) % 4, 0)


def ring_scatter(parts, axis, dim):
    me = lax.axis_index(axis)

    def piece(k):
        return lax.dynamic_index_in_dim(parts, k % 4, dim, keepdims=False).astype(jnp.float32)

    got = shift(piece(me + 2).astype(jnp.bfloat16), axis, 4, 1).astype(jnp.float32)
    up = (piece(me + 1) + got).astype(jnp.bfloat16)
    down = piece(me + 3).astype(jnp.bfloat16)
    up, down = lax.optimization_barrier((up, down))
    acc = piece(me)
    acc = acc + shift(up, axis, 4, 1).astype(jnp.float32)
    return acc + shift(down, axis, 4, -1).astype(jnp.float32)


def scatter_axis(parts, axis, size, dim, relay=False):
    if relay and size == 4:
        return ring_scatter(parts, axis, dim)
    me = lax.axis_index(axis)
    acc = lax.dynamic_index_in_dim(parts, me, dim, keepdims=False).astype(jnp.float32)
    for step in range(1, size):
        out = lax.dynamic_index_in_dim(parts, (me + step) % size, dim, keepdims=False)
        acc = acc + shift(out.astype(jnp.bfloat16), axis, size, step).astype(jnp.float32)
    return acc


def dot_rows(left, right):
    return lax.dot_general(
        left, right, (((1,), (1,)), ((), ())), preferred_element_type=jnp.float32
    )


def dot_cols(left, right):
    return lax.dot_general(
        left, right, (((0,), (0,)), ((), ())), preferred_element_type=jnp.float32
    )


def band_backward(query_block, key_band, value_band, grad_block, query_start, key_start):
    length = query_block.shape[0]
    span = key_band.shape[0]
    query_pos = query_start + jnp.arange(length, dtype=jnp.int32)
    key_pos = key_start + jnp.arange(span, dtype=jnp.int32)
    offset = query_pos[:, None] - key_pos[None, :]
    allowed = (key_pos[None, :] >= 0) & (offset >= 0) & (offset < WINDOW)
    scores = dot_rows(query_block, key_band) * score_scale
    masked = jnp.where(allowed, scores, -1e30)
    top = jnp.max(masked, axis=1, keepdims=True)
    weights = jnp.where(allowed, jnp.exp(masked - top), 0.0)
    probs = weights / jnp.sum(weights, axis=1, keepdims=True)
    probs_low = probs.astype(jnp.bfloat16)
    grad_probs = dot_rows(grad_block, value_band)
    delta = jnp.sum(probs * grad_probs, axis=1, keepdims=True)
    grad_scores = (probs * (grad_probs - delta)).astype(jnp.bfloat16)
    grad_query = (
        jnp.dot(grad_scores, key_band, preferred_element_type=jnp.float32) * score_scale
    ).astype(jnp.bfloat16)
    grad_keys = (dot_cols(grad_scores, query_block) * score_scale).astype(jnp.bfloat16)
    grad_values = dot_cols(probs_low, grad_block).astype(jnp.bfloat16)
    return (grad_query, grad_keys, grad_values)


def make_body(n_zhi, n_x, n_core):
    def body(query, keys, values, d_out, w_out, w_query, w_key, w_value):
        length, dim = query.shape
        width = d_out.shape[1]
        seq_index = lax.axis_index("seq")
        stacked = gather_axis(d_out, "zhi", n_zhi, relay=True)
        stacked = gather_axis(stacked, "x", n_x)
        stacked = gather_axis(stacked, "core", n_core)
        out_rows = w_out.reshape(w_out.shape[0], n_zhi, n_x, n_core, width)
        grad_heads = jnp.einsum(
            "cxzti,hzxci->th", stacked, out_rows, preferred_element_type=jnp.float32
        ).astype(jnp.bfloat16)
        reach = NBR
        kv = jnp.concatenate([keys, values], axis=1)
        kv_blocks = [from_behind(kv, "seq", distance) for distance in range(reach, 0, -1)]
        kv_band = jnp.concatenate(kv_blocks + [kv], axis=0)
        key_band = kv_band[:, :dim]
        value_band = kv_band[:, dim:]
        query_start = seq_index * length
        grad_query, key_parts, value_parts = band_backward(
            query, key_band, value_band, grad_heads, query_start, query_start - reach * length
        )
        kv_parts = jnp.concatenate([key_parts, value_parts], axis=1)
        kv_total = kv_parts[reach * length :].astype(jnp.float32)
        for distance in range(1, reach + 1):
            first = (reach - distance) * length
            back = from_behind(kv_parts[first : first + length], "seq", -distance)
            kv_total = kv_total + back.astype(jnp.float32)
        kv_total = kv_total.astype(jnp.bfloat16)
        grad_keys = kv_total[:, :dim]
        grad_values = kv_total[:, dim:]
        core_index = lax.axis_index("core")

        def project(index):
            def rows(w):
                w = w.reshape(n_zhi, n_x, n_core, width, dim)
                return lax.dynamic_index_in_dim(w, index, 2, keepdims=False).reshape(-1, dim)

            summed = dot_rows(rows(w_query), grad_query)
            summed = summed + dot_rows(rows(w_key), grad_keys)
            summed = summed + dot_rows(rows(w_value), grad_values)
            return summed.astype(jnp.bfloat16).reshape(n_zhi, n_x, width, length)

        keep = project(core_index)
        sent = shift(project((core_index + 1) % n_core), "core", n_core, 1)
        part = keep.astype(jnp.float32) + sent.astype(jnp.float32)
        part = scatter_axis(part, "x", n_x, 1)
        part = scatter_axis(part, "zhi", n_zhi, 0, relay=True)
        return part.T.astype(jnp.bfloat16)

    return body


def solution(mesh):
    n_seq, n_head = mesh.devices.shape
    n_core = 2
    n_x = len({d.coords[0] for d in mesh.devices[0]})
    n_zhi = n_head // (n_x * n_core)
    fine = Mesh(mesh.devices.reshape(n_seq, n_zhi, n_x, n_core), ("seq", "zhi", "x", "core"))
    head = ("zhi", "x", "core")
    in_specs = (
        P("seq", head),
        P("seq", head),
        P("seq", head),
        P("seq", head),
        P(head, None),
        P(None, head),
        P(None, head),
        P(None, head),
    )
    out_specs = P("seq", head)
    return jax.shard_map(
        make_body(n_zhi, n_x, n_core),
        mesh=fine,
        in_specs=in_specs,
        out_specs=out_specs,
        check_vma=False,
    )
```

```python
import jax
import jax.numpy as jnp
from jax import lax
from jax.sharding import Mesh
from jax.sharding import PartitionSpec as P

WINDOW = 1024
NBR = 4


score_scale = 168.0 ** (-0.5)


def from_behind(block, axis, distance):
    devices = range(lax.axis_size(axis))
    route = [(i - distance, i) for i in devices if i - distance in devices]
    return lax.ppermute(block, axis, route)


def shift(block, axis, size, step):
    return lax.ppermute(block, axis, [(i, (i + step) % size) for i in range(size)])


def gather_axis(block, axis, size, relay=False):
    if relay and size == 4:
        return ring_gather(block, axis)
    me = lax.axis_index(axis)
    buf = jnp.zeros((size,) + block.shape, block.dtype)
    buf = lax.dynamic_update_index_in_dim(buf, block, me, 0)
    for step in range(1, size):
        got = shift(block, axis, size, step)
        buf = lax.dynamic_update_index_in_dim(buf, got, (me - step) % size, 0)
    return buf


def ring_gather(block, axis):
    me = lax.axis_index(axis)
    ahead = shift(block, axis, 4, 1)
    behind = shift(block, axis, 4, -1)
    far = shift(ahead, axis, 4, 1)
    buf = jnp.zeros((4,) + block.shape, block.dtype)
    buf = lax.dynamic_update_index_in_dim(buf, block, me, 0)
    buf = lax.dynamic_update_index_in_dim(buf, ahead, (me + 3) % 4, 0)
    buf = lax.dynamic_update_index_in_dim(buf, behind, (me + 1) % 4, 0)
    return lax.dynamic_update_index_in_dim(buf, far, (me + 2) % 4, 0)


def ring_scatter(parts, axis, dim):
    me = lax.axis_index(axis)

    def piece(k):
        return lax.dynamic_index_in_dim(parts, k % 4, dim, keepdims=False).astype(jnp.float32)

    got = shift(piece(me + 2).astype(jnp.bfloat16), axis, 4, 1).astype(jnp.float32)
    up = (piece(me + 1) + got).astype(jnp.bfloat16)
    down = piece(me + 3).astype(jnp.bfloat16)
    acc = piece(me)
    acc = acc + shift(up, axis, 4, 1).astype(jnp.float32)
    return acc + shift(down, axis, 4, -1).astype(jnp.float32)


def scatter_axis(parts, axis, size, dim, relay=False):
    if relay and size == 4:
        return ring_scatter(parts, axis, dim)
    me = lax.axis_index(axis)
    acc = lax.dynamic_index_in_dim(parts, me, dim, keepdims=False).astype(jnp.float32)
    for step in range(1, size):
        out = lax.dynamic_index_in_dim(parts, (me + step) % size, dim, keepdims=False)
        acc = acc + shift(out.astype(jnp.bfloat16), axis, size, step).astype(jnp.float32)
    return acc


def dot_rows(left, right):
    return lax.dot_general(
        left, right, (((1,), (1,)), ((), ())), preferred_element_type=jnp.float32
    )


def dot_cols(left, right):
    return lax.dot_general(
        left, right, (((0,), (0,)), ((), ())), preferred_element_type=jnp.float32
    )


def band_backward(query_block, key_band, value_band, grad_block, query_start, key_start):
    length = query_block.shape[0]
    span = key_band.shape[0]
    query_pos = query_start + jnp.arange(length, dtype=jnp.int32)
    key_pos = key_start + jnp.arange(span, dtype=jnp.int32)
    offset = query_pos[:, None] - key_pos[None, :]
    allowed = (key_pos[None, :] >= 0) & (offset >= 0) & (offset < WINDOW)
    scores = dot_rows(query_block, key_band) * score_scale
    masked = jnp.where(allowed, scores, -1e30)
    top = jnp.max(masked, axis=1, keepdims=True)
    weights = jnp.where(allowed, jnp.exp(masked - top), 0.0)
    probs = weights / jnp.sum(weights, axis=1, keepdims=True)
    probs_low = probs.astype(jnp.bfloat16)
    grad_probs = dot_rows(grad_block, value_band)
    delta = jnp.sum(probs * grad_probs, axis=1, keepdims=True)
    grad_scores = (probs * (grad_probs - delta)).astype(jnp.bfloat16)
    grad_query = (
        jnp.dot(grad_scores, key_band, preferred_element_type=jnp.float32) * score_scale
    ).astype(jnp.bfloat16)
    grad_keys = (dot_cols(grad_scores, query_block) * score_scale).astype(jnp.bfloat16)
    grad_values = dot_cols(probs_low, grad_block).astype(jnp.bfloat16)
    return (grad_query, grad_keys, grad_values)


def make_body(n_zhi, n_x, n_core):
    def body(query, keys, values, d_out, w_out, w_query, w_key, w_value):
        length, dim = query.shape
        width = d_out.shape[1]
        seq_index = lax.axis_index("seq")
        stacked = gather_axis(d_out, "zhi", n_zhi, relay=True)
        stacked = gather_axis(stacked, "x", n_x)
        stacked = gather_axis(stacked, "core", n_core)
        out_rows = w_out.reshape(w_out.shape[0], n_zhi, n_x, n_core, width)
        grad_heads = jnp.einsum(
            "cxzti,hzxci->th", stacked, out_rows, preferred_element_type=jnp.float32
        ).astype(jnp.bfloat16)
        reach = NBR
        kv = jnp.concatenate([keys, values], axis=1)
        kv_blocks = [from_behind(kv, "seq", distance) for distance in range(reach, 0, -1)]
        kv_band = jnp.concatenate(kv_blocks + [kv], axis=0)
        key_band = kv_band[:, :dim]
        value_band = kv_band[:, dim:]
        query_start = seq_index * length
        grad_query, key_parts, value_parts = band_backward(
            query, key_band, value_band, grad_heads, query_start, query_start - reach * length
        )
        kv_parts = jnp.concatenate([key_parts, value_parts], axis=1)
        core_index = lax.axis_index("core")
        given = lax.dynamic_slice_in_dim(kv_parts, (1 - core_index) * dim, dim, 1)
        pair = lax.dynamic_slice_in_dim(kv_parts, core_index * dim, dim, 1).astype(jnp.float32)
        pair = (pair + shift(given, "core", n_core, 1).astype(jnp.float32)).astype(jnp.bfloat16)
        total = pair[reach * length :].astype(jnp.float32)
        for distance in range(1, reach + 1):
            first = (reach - distance) * length
            back = from_behind(pair[first : first + length], "seq", -distance)
            total = total + back.astype(jnp.float32)
        grad_pair = total.astype(jnp.bfloat16)
        w_pair = lax.select(core_index == 0, w_key, w_value)

        def project(index):
            def rows(w):
                w = w.reshape(n_zhi, n_x, n_core, width, dim)
                return lax.dynamic_index_in_dim(w, index, 2, keepdims=False).reshape(-1, dim)

            summed = dot_rows(rows(w_query), grad_query)
            summed = summed + dot_rows(rows(w_pair), grad_pair)
            return summed.astype(jnp.bfloat16).reshape(n_zhi, n_x, width, length)

        keep = project(core_index)
        sent = shift(project((core_index + 1) % n_core), "core", n_core, 1)
        part = keep.astype(jnp.float32) + sent.astype(jnp.float32)
        part = scatter_axis(part, "x", n_x, 1)
        part = scatter_axis(part, "zhi", n_zhi, 0, relay=True)
        return part.T.astype(jnp.bfloat16)

    return body


def solution(mesh):
    n_seq, n_head = mesh.devices.shape
    n_core = 2
    n_x = len({d.coords[0] for d in mesh.devices[0]})
    n_zhi = n_head // (n_x * n_core)
    fine = Mesh(mesh.devices.reshape(n_seq, n_zhi, n_x, n_core), ("seq", "zhi", "x", "core"))
    head = ("zhi", "x", "core")
    in_specs = (
        P("seq", head),
        P("seq", head),
        P("seq", head),
        P("seq", head),
        P(head, None),
        P(None, head),
        P(None, head),
        P(None, head),
    )
    out_specs = P("seq", head)
    return jax.shard_map(
        make_body(n_zhi, n_x, n_core),
        mesh=fine,
        in_specs=in_specs,
        out_specs=out_specs,
        check_vma=False,
    )
```

```python
import jax
import jax.numpy as jnp
from jax import lax
from jax.sharding import Mesh
from jax.sharding import PartitionSpec as P

WINDOW = 1024
NBR = 4


score_scale = 168.0 ** (-0.5)


def from_behind(block, axis, distance):
    devices = range(lax.axis_size(axis))
    route = [(i - distance, i) for i in devices if i - distance in devices]
    return lax.ppermute(block, axis, route)


def shift(block, axis, size, step):
    return lax.ppermute(block, axis, [(i, (i + step) % size) for i in range(size)])


def gather_axis(block, axis, size, relay=False):
    if relay and size == 4:
        return ring_gather(block, axis)
    me = lax.axis_index(axis)
    buf = jnp.zeros((size,) + block.shape, block.dtype)
    buf = lax.dynamic_update_index_in_dim(buf, block, me, 0)
    for step in range(1, size):
        got = shift(block, axis, size, step)
        buf = lax.dynamic_update_index_in_dim(buf, got, (me - step) % size, 0)
    return buf


def ring_gather(block, axis):
    me = lax.axis_index(axis)
    ahead = shift(block, axis, 4, 1)
    behind = shift(block, axis, 4, -1)
    far = shift(ahead, axis, 4, 1)
    buf = jnp.zeros((4,) + block.shape, block.dtype)
    buf = lax.dynamic_update_index_in_dim(buf, block, me, 0)
    buf = lax.dynamic_update_index_in_dim(buf, ahead, (me + 3) % 4, 0)
    buf = lax.dynamic_update_index_in_dim(buf, behind, (me + 1) % 4, 0)
    return lax.dynamic_update_index_in_dim(buf, far, (me + 2) % 4, 0)


def ring_scatter(parts, axis, dim):
    me = lax.axis_index(axis)

    def piece(k):
        return lax.dynamic_index_in_dim(parts, k % 4, dim, keepdims=False).astype(jnp.float32)

    got = shift(piece(me + 2).astype(jnp.bfloat16), axis, 4, 1).astype(jnp.float32)
    up = (piece(me + 1) + got).astype(jnp.bfloat16)
    down = piece(me + 3).astype(jnp.bfloat16)
    acc = piece(me)
    acc = acc + shift(up, axis, 4, 1).astype(jnp.float32)
    return acc + shift(down, axis, 4, -1).astype(jnp.float32)


def scatter_axis(parts, axis, size, dim, relay=False):
    if relay and size == 4:
        return ring_scatter(parts, axis, dim)
    me = lax.axis_index(axis)
    acc = lax.dynamic_index_in_dim(parts, me, dim, keepdims=False).astype(jnp.float32)
    for step in range(1, size):
        out = lax.dynamic_index_in_dim(parts, (me + step) % size, dim, keepdims=False)
        acc = acc + shift(out.astype(jnp.bfloat16), axis, size, step).astype(jnp.float32)
    return acc


def dot_rows(left, right):
    return lax.dot_general(
        left, right, (((1,), (1,)), ((), ())), preferred_element_type=jnp.float32
    )


def dot_cols(left, right):
    return lax.dot_general(
        left, right, (((0,), (0,)), ((), ())), preferred_element_type=jnp.float32
    )


def band_probs(query_block, key_band, query_start, key_start):
    length = query_block.shape[0]
    span = key_band.shape[0]
    query_pos = query_start + jnp.arange(length, dtype=jnp.int32)
    key_pos = key_start + jnp.arange(span, dtype=jnp.int32)
    offset = query_pos[:, None] - key_pos[None, :]
    allowed = (key_pos[None, :] >= 0) & (offset >= 0) & (offset < WINDOW)
    scores = dot_rows(query_block, key_band) * score_scale
    masked = jnp.where(allowed, scores, -1e30)
    top = jnp.max(masked, axis=1, keepdims=True)
    weights = jnp.where(allowed, jnp.exp(masked - top), 0.0)
    probs = weights / jnp.sum(weights, axis=1, keepdims=True)
    return probs


def band_backward(query_block, key_band, value_band, grad_block, probs):
    probs_low = probs.astype(jnp.bfloat16)
    grad_probs = dot_rows(grad_block, value_band)
    delta = jnp.sum(probs * grad_probs, axis=1, keepdims=True)
    grad_scores = (probs * (grad_probs - delta)).astype(jnp.bfloat16)
    grad_query = (
        jnp.dot(grad_scores, key_band, preferred_element_type=jnp.float32) * score_scale
    ).astype(jnp.bfloat16)
    grad_keys = (dot_cols(grad_scores, query_block) * score_scale).astype(jnp.bfloat16)
    grad_values = dot_cols(probs_low, grad_block).astype(jnp.bfloat16)
    return (grad_query, grad_keys, grad_values)


def make_body(n_zhi, n_x, n_core):
    def body(query, keys, values, d_out, w_out, w_query, w_key, w_value):
        length, dim = query.shape
        width = d_out.shape[1]
        seq_index = lax.axis_index("seq")
        stacked = gather_axis(d_out, "zhi", n_zhi, relay=True)
        reach = NBR
        kv = jnp.concatenate([keys, values], axis=1)
        kv_blocks = [from_behind(kv, "seq", distance) for distance in range(reach, 0, -1)]
        kv_band = jnp.concatenate(kv_blocks + [kv], axis=0)
        query_start = seq_index * length
        probs = band_probs(query, kv_band[:, :dim], query_start, query_start - reach * length)
        stacked, kv_band, probs = lax.optimization_barrier((stacked, kv_band, probs))
        stacked = gather_axis(stacked, "x", n_x)
        stacked = gather_axis(stacked, "core", n_core)
        out_rows = w_out.reshape(w_out.shape[0], n_zhi, n_x, n_core, width)
        grad_heads = jnp.einsum(
            "cxzti,hzxci->th", stacked, out_rows, preferred_element_type=jnp.float32
        ).astype(jnp.bfloat16)
        key_band = kv_band[:, :dim]
        value_band = kv_band[:, dim:]
        grad_query, key_parts, value_parts = band_backward(
            query, key_band, value_band, grad_heads, probs
        )
        kv_parts = jnp.concatenate([key_parts, value_parts], axis=1)
        kv_total = kv_parts[reach * length :].astype(jnp.float32)
        for distance in range(1, reach + 1):
            first = (reach - distance) * length
            back = from_behind(kv_parts[first : first + length], "seq", -distance)
            kv_total = kv_total + back.astype(jnp.float32)
        kv_total = kv_total.astype(jnp.bfloat16)
        grad_keys = kv_total[:, :dim]
        grad_values = kv_total[:, dim:]
        core_index = lax.axis_index("core")

        def project(index):
            def rows(w):
                w = w.reshape(n_zhi, n_x, n_core, width, dim)
                return lax.dynamic_index_in_dim(w, index, 2, keepdims=False).reshape(-1, dim)

            summed = dot_rows(rows(w_query), grad_query)
            summed = summed + dot_rows(rows(w_key), grad_keys)
            summed = summed + dot_rows(rows(w_value), grad_values)
            return summed.astype(jnp.bfloat16).reshape(n_zhi, n_x, width, length)

        keep = project(core_index)
        sent = shift(project((core_index + 1) % n_core), "core", n_core, 1)
        part = keep.astype(jnp.float32) + sent.astype(jnp.float32)
        part = scatter_axis(part, "x", n_x, 1)
        part = scatter_axis(part, "zhi", n_zhi, 0, relay=True)
        return part.T.astype(jnp.bfloat16)

    return body


def solution(mesh):
    n_seq, n_head = mesh.devices.shape
    n_core = 2
    n_x = len({d.coords[0] for d in mesh.devices[0]})
    n_zhi = n_head // (n_x * n_core)
    fine = Mesh(mesh.devices.reshape(n_seq, n_zhi, n_x, n_core), ("seq", "zhi", "x", "core"))
    head = ("zhi", "x", "core")
    in_specs = (
        P("seq", head),
        P("seq", head),
        P("seq", head),
        P("seq", head),
        P(head, None),
        P(None, head),
        P(None, head),
        P(None, head),
    )
    out_specs = P("seq", head)
    return jax.shard_map(
        make_body(n_zhi, n_x, n_core),
        mesh=fine,
        in_specs=in_specs,
        out_specs=out_specs,
        check_vma=False,
    )
```

```python
import jax
import jax.numpy as jnp
from jax import lax
from jax.sharding import Mesh
from jax.sharding import PartitionSpec as P

WINDOW = 1024
NBR = 4


score_scale = 168.0 ** (-0.5)


def from_behind(block, axis, distance):
    devices = range(lax.axis_size(axis))
    route = [(i - distance, i) for i in devices if i - distance in devices]
    return lax.ppermute(block, axis, route)


def shift(block, axis, size, step):
    return lax.ppermute(block, axis, [(i, (i + step) % size) for i in range(size)])


def gather_axis(block, axis, size, relay=False):
    if relay and size == 4:
        return ring_gather(block, axis)
    me = lax.axis_index(axis)
    buf = jnp.zeros((size,) + block.shape, block.dtype)
    buf = lax.dynamic_update_index_in_dim(buf, block, me, 0)
    for step in range(1, size):
        got = shift(block, axis, size, step)
        buf = lax.dynamic_update_index_in_dim(buf, got, (me - step) % size, 0)
    return buf


def ring_gather(block, axis):
    me = lax.axis_index(axis)
    ahead = shift(block, axis, 4, 1)
    behind = shift(block, axis, 4, -1)
    far = shift(ahead, axis, 4, 1)
    buf = jnp.zeros((4,) + block.shape, block.dtype)
    buf = lax.dynamic_update_index_in_dim(buf, block, me, 0)
    buf = lax.dynamic_update_index_in_dim(buf, ahead, (me + 3) % 4, 0)
    buf = lax.dynamic_update_index_in_dim(buf, behind, (me + 1) % 4, 0)
    return lax.dynamic_update_index_in_dim(buf, far, (me + 2) % 4, 0)


def ring_scatter(parts, axis, dim):
    me = lax.axis_index(axis)

    def piece(k):
        return lax.dynamic_index_in_dim(parts, k % 4, dim, keepdims=False).astype(jnp.float32)

    got = shift(piece(me + 2).astype(jnp.bfloat16), axis, 4, 1).astype(jnp.float32)
    up = (piece(me + 1) + got).astype(jnp.bfloat16)
    down = piece(me + 3).astype(jnp.bfloat16)
    acc = piece(me)
    acc = acc + shift(up, axis, 4, 1).astype(jnp.float32)
    return acc + shift(down, axis, 4, -1).astype(jnp.float32)


def scatter_axis(parts, axis, size, dim, relay=False):
    if relay and size == 4:
        return ring_scatter(parts, axis, dim)
    me = lax.axis_index(axis)
    acc = lax.dynamic_index_in_dim(parts, me, dim, keepdims=False).astype(jnp.float32)
    for step in range(1, size):
        out = lax.dynamic_index_in_dim(parts, (me + step) % size, dim, keepdims=False)
        acc = acc + shift(out.astype(jnp.bfloat16), axis, size, step).astype(jnp.float32)
    return acc


def dot_rows(left, right):
    return lax.dot_general(
        left, right, (((1,), (1,)), ((), ())), preferred_element_type=jnp.float32
    )


def dot_cols(left, right):
    return lax.dot_general(
        left, right, (((0,), (0,)), ((), ())), preferred_element_type=jnp.float32
    )


def band_probs(query_block, key_band, query_start, key_start):
    length = query_block.shape[0]
    span = key_band.shape[0]
    query_pos = query_start + jnp.arange(length, dtype=jnp.int32)
    key_pos = key_start + jnp.arange(span, dtype=jnp.int32)
    offset = query_pos[:, None] - key_pos[None, :]
    allowed = (key_pos[None, :] >= 0) & (offset >= 0) & (offset < WINDOW)
    scores = dot_rows(query_block, key_band) * score_scale
    masked = jnp.where(allowed, scores, -1e30)
    top = jnp.max(masked, axis=1, keepdims=True)
    weights = jnp.where(allowed, jnp.exp(masked - top), 0.0)
    probs = weights / jnp.sum(weights, axis=1, keepdims=True)
    return probs


def band_backward(query_block, key_band, value_band, grad_block, probs):
    probs_low = probs.astype(jnp.bfloat16)
    grad_probs = dot_rows(grad_block, value_band)
    delta = jnp.sum(probs * grad_probs, axis=1, keepdims=True)
    grad_scores = (probs * (grad_probs - delta)).astype(jnp.bfloat16)
    grad_query = (
        jnp.dot(grad_scores, key_band, preferred_element_type=jnp.float32) * score_scale
    ).astype(jnp.bfloat16)
    grad_keys = (dot_cols(grad_scores, query_block) * score_scale).astype(jnp.bfloat16)
    grad_values = dot_cols(probs_low, grad_block).astype(jnp.bfloat16)
    return (grad_query, grad_keys, grad_values)


def make_body(n_zhi, n_x, n_core):
    def body(query, keys, values, d_out, w_out, w_query, w_key, w_value):
        length, dim = query.shape
        width = d_out.shape[1]
        seq_index = lax.axis_index("seq")
        stacked = gather_axis(d_out, "zhi", n_zhi, relay=True)
        reach = NBR
        kv = jnp.concatenate([keys, values], axis=1)
        kv_blocks = [from_behind(kv, "seq", distance) for distance in range(reach, 0, -1)]
        kv_band = jnp.concatenate(kv_blocks + [kv], axis=0)
        query_start = seq_index * length
        probs = band_probs(query, kv_band[:, :dim], query_start, query_start - reach * length)
        stacked, kv_band, probs = lax.optimization_barrier((stacked, kv_band, probs))
        stacked = gather_axis(stacked, "x", n_x)
        stacked = gather_axis(stacked, "core", n_core)
        out_rows = w_out.reshape(w_out.shape[0], n_zhi, n_x, n_core, width)
        grad_heads = jnp.einsum(
            "cxzti,hzxci->th", stacked, out_rows, preferred_element_type=jnp.float32
        ).astype(jnp.bfloat16)
        key_band = kv_band[:, :dim]
        value_band = kv_band[:, dim:]
        grad_query, key_parts, value_parts = band_backward(
            query, key_band, value_band, grad_heads, probs
        )
        kv_parts = jnp.concatenate([key_parts, value_parts], axis=1)
        kv_total = kv_parts[reach * length :].astype(jnp.float32)
        for distance in range(1, reach + 1):
            first = (reach - distance) * length
            back = from_behind(kv_parts[first : first + length], "seq", -distance)
            kv_total = kv_total + back.astype(jnp.float32)
        kv_total = kv_total.astype(jnp.bfloat16)
        grad_keys = kv_total[:, :dim]
        grad_values = kv_total[:, dim:]
        core_index = lax.axis_index("core")

        def project(index):
            def rows(w):
                w = w.reshape(n_zhi, n_x, n_core, width, dim)
                return lax.dynamic_index_in_dim(w, index, 2, keepdims=False).reshape(-1, dim)

            summed = dot_rows(rows(w_query), grad_query)
            summed = summed + dot_rows(rows(w_key), grad_keys)
            summed = summed + dot_rows(rows(w_value), grad_values)
            return summed.astype(jnp.bfloat16).reshape(n_zhi, n_x, width, length)

        keep = project(core_index)
        sent = shift(project((core_index + 1) % n_core), "core", n_core, 1)
        part = keep.astype(jnp.float32) + sent.astype(jnp.float32)
        part = scatter_axis(part, "x", n_x, 1, relay=True)
        part = scatter_axis(part, "zhi", n_zhi, 0, relay=True)
        return part.T.astype(jnp.bfloat16)

    return body


def solution(mesh):
    n_seq, n_head = mesh.devices.shape
    n_core = 2
    n_x = len({d.coords[0] for d in mesh.devices[0]})
    n_zhi = n_head // (n_x * n_core)
    fine = Mesh(mesh.devices.reshape(n_seq, n_zhi, n_x, n_core), ("seq", "zhi", "x", "core"))
    head = ("zhi", "x", "core")
    in_specs = (
        P("seq", head),
        P("seq", head),
        P("seq", head),
        P("seq", head),
        P(head, None),
        P(None, head),
        P(None, head),
        P(None, head),
    )
    out_specs = P("seq", head)
    return jax.shard_map(
        make_body(n_zhi, n_x, n_core),
        mesh=fine,
        in_specs=in_specs,
        out_specs=out_specs,
        check_vma=False,
    )
```

```python
import jax
import jax.numpy as jnp
from jax import lax
from jax.sharding import Mesh
from jax.sharding import PartitionSpec as P

WINDOW = 1024
NBR = 4


score_scale = 168.0 ** (-0.5)


def from_behind(block, axis, distance):
    devices = range(lax.axis_size(axis))
    route = [(i - distance, i) for i in devices if i - distance in devices]
    return lax.ppermute(block, axis, route)


def shift(block, axis, size, step):
    return lax.ppermute(block, axis, [(i, (i + step) % size) for i in range(size)])


def gather_axis(block, axis, size, relay=False):
    if relay and size == 4:
        return ring_gather(block, axis)
    me = lax.axis_index(axis)
    buf = jnp.zeros((size,) + block.shape, block.dtype)
    buf = lax.dynamic_update_index_in_dim(buf, block, me, 0)
    for step in range(1, size):
        got = shift(block, axis, size, step)
        buf = lax.dynamic_update_index_in_dim(buf, got, (me - step) % size, 0)
    return buf


def ring_gather(block, axis):
    me = lax.axis_index(axis)
    ahead = shift(block, axis, 4, 1)
    behind = shift(block, axis, 4, -1)
    far = shift(ahead, axis, 4, 1)
    buf = jnp.zeros((4,) + block.shape, block.dtype)
    buf = lax.dynamic_update_index_in_dim(buf, block, me, 0)
    buf = lax.dynamic_update_index_in_dim(buf, ahead, (me + 3) % 4, 0)
    buf = lax.dynamic_update_index_in_dim(buf, behind, (me + 1) % 4, 0)
    return lax.dynamic_update_index_in_dim(buf, far, (me + 2) % 4, 0)


def ring_scatter(parts, axis, dim):
    me = lax.axis_index(axis)

    def piece(k):
        return lax.dynamic_index_in_dim(parts, k % 4, dim, keepdims=False).astype(jnp.float32)

    got = shift(piece(me + 2).astype(jnp.bfloat16), axis, 4, 1).astype(jnp.float32)
    up = (piece(me + 1) + got).astype(jnp.bfloat16)
    down = piece(me + 3).astype(jnp.bfloat16)
    acc = piece(me)
    acc = acc + shift(up, axis, 4, 1).astype(jnp.float32)
    return acc + shift(down, axis, 4, -1).astype(jnp.float32)


def scatter_axis(parts, axis, size, dim, relay=False):
    if relay and size == 4:
        return ring_scatter(parts, axis, dim)
    me = lax.axis_index(axis)
    acc = lax.dynamic_index_in_dim(parts, me, dim, keepdims=False).astype(jnp.float32)
    for step in range(1, size):
        out = lax.dynamic_index_in_dim(parts, (me + step) % size, dim, keepdims=False)
        acc = acc + shift(out.astype(jnp.bfloat16), axis, size, step).astype(jnp.float32)
    return acc


def dot_rows(left, right):
    return lax.dot_general(
        left, right, (((1,), (1,)), ((), ())), preferred_element_type=jnp.float32
    )


def dot_cols(left, right):
    return lax.dot_general(
        left, right, (((0,), (0,)), ((), ())), preferred_element_type=jnp.float32
    )


def band_probs(query_block, key_band, query_start, key_start):
    length = query_block.shape[0]
    span = key_band.shape[0]
    query_pos = query_start + jnp.arange(length, dtype=jnp.int32)
    key_pos = key_start + jnp.arange(span, dtype=jnp.int32)
    offset = query_pos[:, None] - key_pos[None, :]
    allowed = (key_pos[None, :] >= 0) & (offset >= 0) & (offset < WINDOW)
    scores = dot_rows(query_block, key_band) * score_scale
    masked = jnp.where(allowed, scores, -1e30)
    top = jnp.max(masked, axis=1, keepdims=True)
    weights = jnp.where(allowed, jnp.exp(masked - top), 0.0)
    probs = weights / jnp.sum(weights, axis=1, keepdims=True)
    return probs


def band_backward(query_block, key_band, value_band, grad_block, probs):
    probs_low = probs.astype(jnp.bfloat16)
    grad_probs = dot_rows(grad_block, value_band)
    delta = jnp.sum(probs * grad_probs, axis=1, keepdims=True)
    grad_scores = (probs * (grad_probs - delta)).astype(jnp.bfloat16)
    grad_query = (
        jnp.dot(grad_scores, key_band, preferred_element_type=jnp.float32) * score_scale
    ).astype(jnp.bfloat16)
    grad_keys = (dot_cols(grad_scores, query_block) * score_scale).astype(jnp.bfloat16)
    grad_values = dot_cols(probs_low, grad_block).astype(jnp.bfloat16)
    return (grad_query, grad_keys, grad_values)


def make_body(n_zhi, n_x, n_core):
    def body(query, keys, values, d_out, w_out, w_query, w_key, w_value):
        length, dim = query.shape
        width = d_out.shape[1]
        seq_index = lax.axis_index("seq")
        stacked = gather_axis(d_out, "zhi", n_zhi, relay=True)
        reach = NBR
        kv = jnp.concatenate([keys, values], axis=1)
        kv_blocks = [from_behind(kv, "seq", distance) for distance in range(reach, 0, -1)]
        kv_band = jnp.concatenate(kv_blocks + [kv], axis=0)
        query_start = seq_index * length
        probs = band_probs(query, kv_band[:, :dim], query_start, query_start - reach * length)
        stacked, kv_band, probs = lax.optimization_barrier((stacked, kv_band, probs))
        stacked = gather_axis(stacked, "x", n_x, relay=True)
        stacked = gather_axis(stacked, "core", n_core)
        out_rows = w_out.reshape(w_out.shape[0], n_zhi, n_x, n_core, width)
        grad_heads = jnp.einsum(
            "cxzti,hzxci->th", stacked, out_rows, preferred_element_type=jnp.float32
        ).astype(jnp.bfloat16)
        key_band = kv_band[:, :dim]
        value_band = kv_band[:, dim:]
        grad_query, key_parts, value_parts = band_backward(
            query, key_band, value_band, grad_heads, probs
        )
        kv_parts = jnp.concatenate([key_parts, value_parts], axis=1)
        kv_total = kv_parts[reach * length :].astype(jnp.float32)
        for distance in range(1, reach + 1):
            first = (reach - distance) * length
            back = from_behind(kv_parts[first : first + length], "seq", -distance)
            kv_total = kv_total + back.astype(jnp.float32)
        kv_total = kv_total.astype(jnp.bfloat16)
        grad_keys = kv_total[:, :dim]
        grad_values = kv_total[:, dim:]
        core_index = lax.axis_index("core")

        def project(index):
            def rows(w):
                w = w.reshape(n_zhi, n_x, n_core, width, dim)
                return lax.dynamic_index_in_dim(w, index, 2, keepdims=False).reshape(-1, dim)

            summed = dot_rows(rows(w_query), grad_query)
            summed = summed + dot_rows(rows(w_key), grad_keys)
            summed = summed + dot_rows(rows(w_value), grad_values)
            return summed.astype(jnp.bfloat16).reshape(n_zhi, n_x, width, length)

        keep = project(core_index)
        sent = shift(project((core_index + 1) % n_core), "core", n_core, 1)
        part = keep.astype(jnp.float32) + sent.astype(jnp.float32)
        part = scatter_axis(part, "x", n_x, 1)
        part = scatter_axis(part, "zhi", n_zhi, 0, relay=True)
        return part.T.astype(jnp.bfloat16)

    return body


def solution(mesh):
    n_seq, n_head = mesh.devices.shape
    n_core = 2
    n_x = len({d.coords[0] for d in mesh.devices[0]})
    n_zhi = n_head // (n_x * n_core)
    fine = Mesh(mesh.devices.reshape(n_seq, n_zhi, n_x, n_core), ("seq", "zhi", "x", "core"))
    head = ("zhi", "x", "core")
    in_specs = (
        P("seq", head),
        P("seq", head),
        P("seq", head),
        P("seq", head),
        P(head, None),
        P(None, head),
        P(None, head),
        P(None, head),
    )
    out_specs = P("seq", head)
    return jax.shard_map(
        make_body(n_zhi, n_x, n_core),
        mesh=fine,
        in_specs=in_specs,
        out_specs=out_specs,
        check_vma=False,
    )
```
